128 devices in a mesh: row: 8 (over x, core), col: 16 (over y, z).
Axes of the slice: x: 4, y: 4, z: 4, core: 2. Of those that a mesh axis runs over, the one named last changes fastest.
Arguments:
- kernel: float32 [16384, 16384], P('row', 'col'), as said below
Outputs:
- schur: float32 [16384, 16384], P('row', 'col')
- panels: float32 [16384, 768], P('row')
Inputs may be any that keep to these rules, and one draw needn't show every extreme that they name: kernel is symmetric and positive definite with smallest eigenvalue of order one.
All inputs are finite; a program needn't handle non-finite values.
Results may differ from the reference program's by a relative error of at most 0.00027.
Values sent between devices are 32-bit elements; how exact they have to be, the bound alone decides.
No kernel may reach another device: no remote copies, remote signals or barrier semaphores. Data moves between devices by JAX's collectives and lax.ppermute only.
A program may use at most 128 MiB of HBM per device.

```python
import jax
import jax.numpy as jnp
from jax import lax

BLOCK = 256
RB = 8
STEPS = 3
CB = 4
NT = 16384
N_ROW = 8
N_COL = 16


def draw_kernel(key, part):
    direction_key = jax.random.fold_in(key, 21)
    shell_key = jax.random.fold_in(key, 22)
    noise_key = jax.random.fold_in(key, 23)
    level_key = jax.random.fold_in(key, 24)
    stored = jnp.arange(NT)
    row_part = stored // (RB * BLOCK)
    row_local = stored % (RB * BLOCK) // BLOCK
    row_global = (row_local * N_ROW + row_part) * BLOCK + stored % BLOCK
    col_part = stored // (CB * BLOCK)
    col_local = stored % (CB * BLOCK) // BLOCK
    col_global = (col_local * N_COL + col_part) * BLOCK + stored % BLOCK
    vectors = jax.random.normal(direction_key, (NT, 3), jnp.float32)
    lengths = jnp.sqrt(vectors[:, 0] * vectors[:, 0] + vectors[:, 1] * vectors[:, 1] + vectors[:, 2] * vectors[:, 2])
    unit = vectors / jnp.maximum(lengths, 0.001)[:, None]
    shells = jax.random.uniform(shell_key, (NT,), jnp.float32)
    levels = jax.random.uniform(level_key, (NT,), jnp.float32)
    unit_rows = unit[row_global]
    unit_cols = unit[col_global]
    cosine = unit_rows[:, 0:1] * unit_cols[None, :, 0]
    cosine = cosine + unit_rows[:, 1:2] * unit_cols[None, :, 1]
    cosine = cosine + unit_rows[:, 2:3] * unit_cols[None, :, 2]
    angular = jnp.exp((cosine * cosine - 1.0) / 0.5)
    radial = jnp.exp(-jnp.abs(shells[row_global][:, None] - shells[col_global][None, :]) / 0.3)
    smooth = angular * radial
    raw = jax.random.normal(noise_key, (NT, NT), jnp.float32)
    symmetric = (raw + raw.T) * (0.70710678 * 0.5 * NT ** (-0.5))
    symmetric = jnp.take(symmetric, row_global, axis=0)
    symmetric = jnp.take(symmetric, col_global, axis=1)
    same = row_global[:, None] == col_global[None, :]
    nugget = jnp.where(same, (1.5 + levels[row_global])[:, None], 0.0)
    matrix = smooth + symmetric + nugget
    return matrix.astype(jnp.float32)


def setup_inputs(seed: int = 0) -> dict:
    keys = jax.random.split(jax.random.key(seed), 2)
    kernel = draw_kernel(jax.random.fold_in(keys[1], 71), 0)
    return {"kernel": kernel}


def to_matrix(stored):
    grid = stored.reshape(N_ROW, RB, BLOCK, N_COL, CB, BLOCK)
    return grid.transpose(1, 0, 2, 4, 3, 5).reshape(NT, NT)

def to_stored(matrix):
    grid = matrix.reshape(RB, N_ROW, BLOCK, CB, N_COL, BLOCK)
    return grid.transpose(1, 0, 2, 4, 3, 5).reshape(NT, NT)

def reference(kernel):
    matrix = to_matrix(kernel)
    block_ids = jnp.arange(NT) // BLOCK
    collected = []
    for step in range(STEPS):
        start = step * BLOCK
        factor = jnp.linalg.cholesky(matrix[start:start + BLOCK, start:start + BLOCK])
        solved = jax.scipy.linalg.solve_triangular(factor, matrix[:, start:start + BLOCK].T, lower=True).T
        tiled = jnp.tile(factor, (NT // BLOCK, 1))
        panel = jnp.where((block_ids > step)[:, None], solved, jnp.where((block_ids == step)[:, None], tiled, jnp.float32(0.0)))
        matrix = matrix - jnp.dot(panel, panel.T, precision=lax.Precision.HIGHEST)
        collected.append(panel)
    keep = (block_ids >= STEPS)[:, None] & (block_ids >= STEPS)[None, :]
    schur = jnp.where(keep, matrix, jnp.float32(0.0))
    panels = jnp.concatenate(collected, axis=1)
    panels = panels.reshape(RB, N_ROW, BLOCK, STEPS * BLOCK).transpose(1, 0, 2, 3).reshape(NT, STEPS * BLOCK)
    return (to_stored(schur), panels)
```

```python
import jax
import jax.numpy as jnp
from jax import lax
from jax.sharding import PartitionSpec as P

BLOCK = 256
STEPS = 3


def gather_corner(kernel, row_index, col_index):
    width = STEPS * BLOCK
    mine = (row_index < STEPS) & (col_index < STEPS)
    piece = jnp.where(mine, kernel[:BLOCK, :BLOCK], jnp.float32(0.0))
    corner = jnp.zeros((width, width), jnp.float32)
    corner = lax.dynamic_update_slice(
        corner, piece, (jnp.minimum(row_index, STEPS - 1) * BLOCK, jnp.minimum(col_index, STEPS - 1) * BLOCK)
    )
    return lax.psum(corner, ("row", "col"))


def gather_columns(kernel, col_index):
    rows = kernel.shape[0]
    mine = col_index < STEPS
    piece = jnp.where(mine, kernel[:, :BLOCK], jnp.float32(0.0))
    band = jnp.zeros((rows, STEPS * BLOCK), jnp.float32)
    band = lax.dynamic_update_slice(band, piece, (0, jnp.minimum(col_index, STEPS - 1) * BLOCK))
    return lax.psum(band, "col")


def gather_rows(kernel, row_index):
    cols = kernel.shape[1]
    mine = row_index < STEPS
    piece = jnp.where(mine, kernel[:BLOCK, :], jnp.float32(0.0))
    band = jnp.zeros((STEPS * BLOCK, cols), jnp.float32)
    band = lax.dynamic_update_slice(band, piece, (jnp.minimum(row_index, STEPS - 1) * BLOCK, 0))
    return lax.psum(band, "row")


def shards(kernel):
    row_count = lax.axis_size("row")
    col_count = lax.axis_size("col")
    row_index = lax.axis_index("row")
    col_index = lax.axis_index("col")
    rows_local, cols_local = kernel.shape
    width = STEPS * BLOCK
    row_ids = jnp.arange(rows_local) // BLOCK * row_count + row_index
    col_ids = jnp.arange(cols_local) // BLOCK * col_count + col_index

    corner = gather_corner(kernel, row_index, col_index)
    band_cols = gather_columns(kernel, col_index)
    band_rows = gather_rows(kernel, row_index)

    factor = jnp.linalg.cholesky(corner)
    inverse = jax.scipy.linalg.solve_triangular(factor, jnp.eye(width, dtype=jnp.float32), lower=True)
    panels = lax.dot_general(
        band_cols, inverse, (((1,), (1,)), ((), ())),
        precision=lax.Precision.HIGHEST, preferred_element_type=jnp.float32,
    )
    across = lax.dot_general(
        band_rows, inverse, (((0,), (1,)), ((), ())),
        precision=lax.Precision.HIGHEST, preferred_element_type=jnp.float32,
    )
    own = lax.dynamic_slice_in_dim(factor, jnp.minimum(row_index, STEPS - 1) * BLOCK, BLOCK, 0)
    head = jnp.where(row_index < STEPS, own, panels[:BLOCK])
    panels = lax.dynamic_update_slice(panels, head, (0, 0))
    update = lax.dot_general(
        panels, across, (((1,), (1,)), ((), ())),
        precision=lax.Precision.HIGHEST, preferred_element_type=jnp.float32,
    )
    keep = (row_ids >= STEPS)[:, None] & (col_ids >= STEPS)[None, :]
    schur = jnp.where(keep, kernel - update, jnp.float32(0.0))
    return (schur, panels)


def solution(mesh):
    return jax.shard_map(
        shards,
        mesh=mesh,
        in_specs=(P("row", "col"),),
        out_specs=(P("row", "col"), P("row", None)),
        check_vma=False,
    )
```

```python
import jax
import jax.numpy as jnp
from jax import lax
from jax.sharding import PartitionSpec as P

BLOCK = 256
STEPS = 3


def gather_corner(kernel, row_index, col_index):
    row_count = lax.axis_size("row")
    col_count = lax.axis_size("col")
    piece = kernel[:BLOCK, :BLOCK]
    heard = [piece]
    for shift in range(1, col_count):
        pairs = [
            (a * col_count + b, a * col_count + (b + shift) % col_count)
            for a in range(STEPS)
            for b in range(STEPS)
        ]
        heard.append(lax.ppermute(piece, ("row", "col"), pairs))
    heard = jnp.stack(heard)
    band = jnp.concatenate(
        [heard[(col_index - b) % col_count] for b in range(STEPS)], axis=1
    )
    heard = [band]
    for shift in range(1, row_count):
        pairs = [
            (a * col_count + q, ((a + shift) % row_count) * col_count + q)
            for a in range(STEPS)
            for q in range(col_count)
        ]
        heard.append(lax.ppermute(band, ("row", "col"), pairs))
    heard = jnp.stack(heard)
    return jnp.concatenate(
        [heard[(row_index - a) % row_count] for a in range(STEPS)], axis=0
    )


def gather_columns(kernel, col_index):
    rows = kernel.shape[0]
    mine = col_index < STEPS
    piece = jnp.where(mine, kernel[:, :BLOCK], jnp.float32(0.0))
    band = jnp.zeros((rows, STEPS * BLOCK), jnp.float32)
    band = lax.dynamic_update_slice(band, piece, (0, jnp.minimum(col_index, STEPS - 1) * BLOCK))
    return lax.psum(band, "col")


def gather_rows(kernel, row_index):
    cols = kernel.shape[1]
    mine = row_index < STEPS
    piece = jnp.where(mine, kernel[:BLOCK, :], jnp.float32(0.0))
    band = jnp.zeros((STEPS * BLOCK, cols), jnp.float32)
    band = lax.dynamic_update_slice(band, piece, (jnp.minimum(row_index, STEPS - 1) * BLOCK, 0))
    return lax.psum(band, "row")


def shards(kernel):
    row_count = lax.axis_size("row")
    col_count = lax.axis_size("col")
    row_index = lax.axis_index("row")
    col_index = lax.axis_index("col")
    rows_local, cols_local = kernel.shape
    width = STEPS * BLOCK
    row_ids = jnp.arange(rows_local) // BLOCK * row_count + row_index
    col_ids = jnp.arange(cols_local) // BLOCK * col_count + col_index

    corner = gather_corner(kernel, row_index, col_index)
    band_cols = gather_columns(kernel, col_index)
    band_rows = gather_rows(kernel, row_index)

    factor = jnp.linalg.cholesky(corner)
    inverse = jax.scipy.linalg.solve_triangular(factor, jnp.eye(width, dtype=jnp.float32), lower=True)
    panels = lax.dot_general(
        band_cols, inverse, (((1,), (1,)), ((), ())),
        precision=lax.Precision.HIGHEST, preferred_element_type=jnp.float32,
    )
    across = lax.dot_general(
        band_rows, inverse, (((0,), (1,)), ((), ())),
        precision=lax.Precision.HIGHEST, preferred_element_type=jnp.float32,
    )
    own = lax.dynamic_slice_in_dim(factor, jnp.minimum(row_index, STEPS - 1) * BLOCK, BLOCK, 0)
    head = jnp.where(row_index < STEPS, own, panels[:BLOCK])
    panels = lax.dynamic_update_slice(panels, head, (0, 0))
    update = lax.dot_general(
        panels, across, (((1,), (1,)), ((), ())),
        precision=lax.Precision.HIGHEST, preferred_element_type=jnp.float32,
    )
    keep = (row_ids >= STEPS)[:, None] & (col_ids >= STEPS)[None, :]
    schur = jnp.where(keep, kernel - update, jnp.float32(0.0))
    return (schur, panels)


def solution(mesh):
    return jax.shard_map(
        shards,
        mesh=mesh,
        in_specs=(P("row", "col"),),
        out_specs=(P("row", "col"), P("row", None)),
        check_vma=False,
    )
```

```python
import jax
import jax.numpy as jnp
from jax import lax
from jax.sharding import PartitionSpec as P

BLOCK = 256
STEPS = 3


def gather_corner(kernel, row_index, col_index):
    row_count = lax.axis_size("row")
    col_count = lax.axis_size("col")
    piece = kernel[:BLOCK, :BLOCK]
    heard = [piece]
    for shift in range(1, col_count):
        pairs = [
            (a * col_count + b, a * col_count + (b + shift) % col_count)
            for a in range(STEPS)
            for b in range(STEPS)
        ]
        heard.append(lax.ppermute(piece, ("row", "col"), pairs))
    heard = jnp.stack(heard)
    band = jnp.concatenate(
        [heard[(col_index - b) % col_count] for b in range(STEPS)], axis=1
    )
    heard = [band]
    for shift in range(1, row_count):
        pairs = [
            (a * col_count + q, ((a + shift) % row_count) * col_count + q)
            for a in range(STEPS)
            for q in range(col_count)
        ]
        heard.append(lax.ppermute(band, ("row", "col"), pairs))
    heard = jnp.stack(heard)
    return jnp.concatenate(
        [heard[(row_index - a) % row_count] for a in range(STEPS)], axis=0
    )


def gather_columns(kernel, col_index):
    rows = kernel.shape[0]
    mine = col_index < STEPS
    piece = jnp.where(mine, kernel[:, :BLOCK], jnp.float32(0.0))
    band = jnp.zeros((rows, STEPS * BLOCK), jnp.float32)
    band = lax.dynamic_update_slice(band, piece, (0, jnp.minimum(col_index, STEPS - 1) * BLOCK))
    return lax.psum(band, "col")


def gather_rows(kernel, row_index):
    cols = kernel.shape[1]
    mine = row_index < STEPS
    piece = jnp.where(mine, kernel[:BLOCK, :], jnp.float32(0.0))
    band = jnp.zeros((STEPS * BLOCK, cols), jnp.float32)
    band = lax.dynamic_update_slice(band, piece, (jnp.minimum(row_index, STEPS - 1) * BLOCK, 0))
    return lax.psum(band, "row")


def mul(a, b, transpose_b=False):
    dims = (((1,), (1 if transpose_b else 0,)), ((), ()))
    return lax.dot_general(a, b, dims, precision=lax.Precision.HIGHEST, preferred_element_type=jnp.float32)


def factor_corner(blocks):
    eye = jnp.eye(BLOCK, dtype=jnp.float32)
    zero = jnp.zeros((BLOCK, BLOCK), jnp.float32)
    lower = [[None] * STEPS for _ in range(STEPS)]
    diag_inv = []
    for k in range(STEPS):
        schur = blocks[k][k]
        for j in range(k):
            schur = schur - mul(lower[k][j], lower[k][j], True)
        lower[k][k] = jnp.linalg.cholesky(schur)
        diag_inv.append(jax.scipy.linalg.solve_triangular(lower[k][k], eye, lower=True))
        for i in range(k + 1, STEPS):
            below = blocks[i][k]
            for j in range(k):
                below = below - mul(lower[i][j], lower[k][j], True)
            lower[i][k] = mul(below, diag_inv[k], True)
    inv = [[None] * STEPS for _ in range(STEPS)]
    for i in range(STEPS):
        inv[i][i] = diag_inv[i]
        for j in range(i - 1, -1, -1):
            acc = mul(lower[i][j], inv[j][j])
            for m in range(j + 1, i):
                acc = acc + mul(lower[i][m], inv[m][j])
            inv[i][j] = -mul(diag_inv[i], acc)
    factor = jnp.concatenate(
        [jnp.concatenate([lower[i][j] if j <= i else zero for j in range(STEPS)], axis=1) for i in range(STEPS)], axis=0
    )
    inverse = jnp.concatenate(
        [jnp.concatenate([inv[i][j] if j <= i else zero for j in range(STEPS)], axis=1) for i in range(STEPS)], axis=0
    )
    return factor, inverse


def shards(kernel):
    row_count = lax.axis_size("row")
    col_count = lax.axis_size("col")
    row_index = lax.axis_index("row")
    col_index = lax.axis_index("col")
    rows_local, cols_local = kernel.shape
    width = STEPS * BLOCK
    row_ids = jnp.arange(rows_local) // BLOCK * row_count + row_index
    col_ids = jnp.arange(cols_local) // BLOCK * col_count + col_index

    corner = gather_corner(kernel, row_index, col_index)
    band_cols = gather_columns(kernel, col_index)
    band_rows = gather_rows(kernel, row_index)

    blocks = [[corner[a * BLOCK:(a + 1) * BLOCK, b * BLOCK:(b + 1) * BLOCK] for b in range(STEPS)] for a in range(STEPS)]
    factor, inverse = factor_corner(blocks)
    panels = lax.dot_general(
        band_cols, inverse, (((1,), (1,)), ((), ())),
        precision=lax.Precision.HIGH, preferred_element_type=jnp.float32,
    )
    across = lax.dot_general(
        band_rows, inverse, (((0,), (1,)), ((), ())),
        precision=lax.Precision.HIGH, preferred_element_type=jnp.float32,
    )
    own = lax.dynamic_slice_in_dim(factor, jnp.minimum(row_index, STEPS - 1) * BLOCK, BLOCK, 0)
    head = jnp.where(row_index < STEPS, own, panels[:BLOCK])
    panels = lax.dynamic_update_slice(panels, head, (0, 0))
    update = lax.dot_general(
        panels, across, (((1,), (1,)), ((), ())),
        precision=lax.Precision.HIGH, preferred_element_type=jnp.float32,
    )
    keep = (row_ids >= STEPS)[:, None] & (col_ids >= STEPS)[None, :]
    schur = jnp.where(keep, kernel - update, jnp.float32(0.0))
    return (schur, panels)


def solution(mesh):
    return jax.shard_map(
        shards,
        mesh=mesh,
        in_specs=(P("row", "col"),),
        out_specs=(P("row", "col"), P("row", None)),
        check_vma=False,
    )
```

```python
import jax
import jax.numpy as jnp
from jax import lax
from jax.sharding import PartitionSpec as P

BLOCK = 256
STEPS = 3


def gather_corner(kernel, row_index, col_index):
    row_count = lax.axis_size("row")
    col_count = lax.axis_size("col")
    piece = kernel[:BLOCK, :BLOCK]
    heard = [piece]
    for shift in range(1, col_count):
        pairs = [
            (a * col_count + b, a * col_count + (b + shift) % col_count)
            for a in range(STEPS)
            for b in range(a + 1)
        ]
        heard.append(lax.ppermute(piece, ("row", "col"), pairs))
    heard = jnp.stack(heard)
    blocks = []
    for a in range(STEPS):
        band = jnp.concatenate([heard[(col_index - b) % col_count] for b in range(a + 1)], axis=1)
        down = [band]
        for shift in range(1, row_count):
            pairs = [(a * col_count + q, ((a + shift) % row_count) * col_count + q) for q in range(col_count)]
            down.append(lax.ppermute(band, ("row", "col"), pairs))
        band = jnp.stack(down)[(row_index - a) % row_count]
        blocks.append([band[:, b * BLOCK:(b + 1) * BLOCK] for b in range(a + 1)])
    return blocks


def gather_columns(kernel, col_index):
    rows = kernel.shape[0]
    mine = col_index < STEPS
    piece = jnp.where(mine, kernel[:, :BLOCK], jnp.float32(0.0))
    band = jnp.zeros((rows, STEPS * BLOCK), jnp.float32)
    band = lax.dynamic_update_slice(band, piece, (0, jnp.minimum(col_index, STEPS - 1) * BLOCK))
    return lax.psum(band, "col")


def gather_rows(kernel, row_index):
    cols = kernel.shape[1]
    mine = row_index < STEPS
    piece = jnp.where(mine, kernel[:BLOCK, :], jnp.float32(0.0))
    band = jnp.zeros((STEPS * BLOCK, cols), jnp.float32)
    band = lax.dynamic_update_slice(band, piece, (jnp.minimum(row_index, STEPS - 1) * BLOCK, 0))
    return lax.psum(band, "row")


def mul(a, b, transpose_b=False):
    dims = (((1,), (1 if transpose_b else 0,)), ((), ()))
    return lax.dot_general(a, b, dims, precision=lax.Precision.HIGHEST, preferred_element_type=jnp.float32)


def factor_corner(blocks):
    eye = jnp.eye(BLOCK, dtype=jnp.float32)
    zero = jnp.zeros((BLOCK, BLOCK), jnp.float32)
    lower = [[None] * STEPS for _ in range(STEPS)]
    diag_inv = []
    for k in range(STEPS):
        schur = blocks[k][k]
        for j in range(k):
            schur = schur - mul(lower[k][j], lower[k][j], True)
        lower[k][k] = jnp.linalg.cholesky(schur)
        diag_inv.append(jax.scipy.linalg.solve_triangular(lower[k][k], eye, lower=True))
        for i in range(k + 1, STEPS):
            below = blocks[i][k]
            for j in range(k):
                below = below - mul(lower[i][j], lower[k][j], True)
            lower[i][k] = mul(below, diag_inv[k], True)
    inv = [[None] * STEPS for _ in range(STEPS)]
    for i in range(STEPS):
        inv[i][i] = diag_inv[i]
        for j in range(i - 1, -1, -1):
            acc = mul(lower[i][j], inv[j][j])
            for m in range(j + 1, i):
                acc = acc + mul(lower[i][m], inv[m][j])
            inv[i][j] = -mul(diag_inv[i], acc)
    factor = jnp.concatenate(
        [jnp.concatenate([lower[i][j] if j <= i else zero for j in range(STEPS)], axis=1) for i in range(STEPS)], axis=0
    )
    inverse = jnp.concatenate(
        [jnp.concatenate([inv[i][j] if j <= i else zero for j in range(STEPS)], axis=1) for i in range(STEPS)], axis=0
    )
    return factor, inverse


def shards(kernel):
    row_count = lax.axis_size("row")
    col_count = lax.axis_size("col")
    row_index = lax.axis_index("row")
    col_index = lax.axis_index("col")
    rows_local, cols_local = kernel.shape
    width = STEPS * BLOCK
    row_ids = jnp.arange(rows_local) // BLOCK * row_count + row_index
    col_ids = jnp.arange(cols_local) // BLOCK * col_count + col_index

    blocks = gather_corner(kernel, row_index, col_index)
    band_cols = gather_columns(kernel, col_index)
    band_rows = gather_rows(kernel, row_index)

    factor, inverse = factor_corner(blocks)
    panels = lax.dot_general(
        band_cols, inverse, (((1,), (1,)), ((), ())),
        precision=lax.Precision.HIGHEST, preferred_element_type=jnp.float32,
    )
    across = lax.dot_general(
        band_rows, inverse, (((0,), (1,)), ((), ())),
        precision=lax.Precision.HIGHEST, preferred_element_type=jnp.float32,
    )
    own = lax.dynamic_slice_in_dim(factor, jnp.minimum(row_index, STEPS - 1) * BLOCK, BLOCK, 0)
    head = jnp.where(row_index < STEPS, own, panels[:BLOCK])
    panels = lax.dynamic_update_slice(panels, head, (0, 0))
    update = lax.dot_general(
        panels, across, (((1,), (1,)), ((), ())),
        precision=lax.Precision.HIGHEST, preferred_element_type=jnp.float32,
    )
    keep = (row_ids >= STEPS)[:, None] & (col_ids >= STEPS)[None, :]
    schur = jnp.where(keep, kernel - update, jnp.float32(0.0))
    return (schur, panels)


def solution(mesh):
    return jax.shard_map(
        shards,
        mesh=mesh,
        in_specs=(P("row", "col"),),
        out_specs=(P("row", "col"), P("row", None)),
        check_vma=False,
    )
```

```python
import jax
import jax.numpy as jnp
from jax import lax
from jax.sharding import PartitionSpec as P

BLOCK = 256
STEPS = 3


def pick(received, index, count, want):
    total = None
    for shift, part in enumerate(received):
        term = jnp.where((index - shift) % count == want, part, jnp.float32(0.0))
        total = term if total is None else total + term
    return total


def gather_corner(kernel, row_index, col_index):
    row_count = lax.axis_size("row")
    col_count = lax.axis_size("col")
    piece = kernel[:BLOCK, :BLOCK]
    heard = [piece]
    for shift in range(1, col_count):
        pairs = [
            (a * col_count + b, a * col_count + (b + shift) % col_count)
            for a in range(STEPS)
            for b in range(a + 1)
        ]
        heard.append(lax.ppermute(piece, ("row", "col"), pairs))
    bands = []
    for a in range(STEPS):
        band = jnp.concatenate([pick(heard, col_index, col_count, b) for b in range(a + 1)], axis=1)
        bands.append(jnp.pad(band, ((0, 0), (0, (STEPS - 1 - a) * BLOCK))))
    groups = [[0], list(range(1, STEPS))]
    blocks = [None] * STEPS
    for group in groups:
        width = (max(group) + 1) * BLOCK
        mine = None
        for a in group:
            term = jnp.where(row_index == a, bands[a][:, :width], jnp.float32(0.0))
            mine = term if mine is None else mine + term
        down = [mine]
        for shift in range(1, row_count):
            pairs = [
                (a * col_count + q, ((a + shift) % row_count) * col_count + q)
                for a in group
                for q in range(col_count)
            ]
            down.append(lax.ppermute(mine, ("row", "col"), pairs))
        for a in group:
            band = pick(down, row_index, row_count, a)
            blocks[a] = [band[:, b * BLOCK:(b + 1) * BLOCK] for b in range(a + 1)]
    return blocks


def gather_columns(kernel, col_index):
    rows = kernel.shape[0]
    mine = col_index < STEPS
    piece = jnp.where(mine, kernel[:, :BLOCK], jnp.float32(0.0))
    band = jnp.zeros((rows, STEPS * BLOCK), jnp.float32)
    band = lax.dynamic_update_slice(band, piece, (0, jnp.minimum(col_index, STEPS - 1) * BLOCK))
    return lax.psum(band, "col")


def gather_rows(kernel, row_index):
    cols = kernel.shape[1]
    mine = row_index < STEPS
    piece = jnp.where(mine, kernel[:BLOCK, :], jnp.float32(0.0))
    band = jnp.zeros((STEPS * BLOCK, cols), jnp.float32)
    band = lax.dynamic_update_slice(band, piece, (jnp.minimum(row_index, STEPS - 1) * BLOCK, 0))
    return lax.psum(band, "row")


def mul(a, b, transpose_b=False):
    dims = (((1,), (1 if transpose_b else 0,)), ((), ()))
    return lax.dot_general(a, b, dims, precision=lax.Precision.HIGHEST, preferred_element_type=jnp.float32)


def factor_corner(blocks):
    eye = jnp.eye(BLOCK, dtype=jnp.float32)
    zero = jnp.zeros((BLOCK, BLOCK), jnp.float32)
    lower = [[None] * STEPS for _ in range(STEPS)]
    diag_inv = []
    for k in range(STEPS):
        schur = blocks[k][k]
        for j in range(k):
            schur = schur - mul(lower[k][j], lower[k][j], True)
        lower[k][k] = jnp.linalg.cholesky(schur)
        diag_inv.append(jax.scipy.linalg.solve_triangular(lower[k][k], eye, lower=True))
        for i in range(k + 1, STEPS):
            below = blocks[i][k]
            for j in range(k):
                below = below - mul(lower[i][j], lower[k][j], True)
            lower[i][k] = mul(below, diag_inv[k], True)
    inv = [[None] * STEPS for _ in range(STEPS)]
    for i in range(STEPS):
        inv[i][i] = diag_inv[i]
        for j in range(i - 1, -1, -1):
            acc = mul(lower[i][j], inv[j][j])
            for m in range(j + 1, i):
                acc = acc + mul(lower[i][m], inv[m][j])
            inv[i][j] = -mul(diag_inv[i], acc)
    factor = jnp.concatenate(
        [jnp.concatenate([lower[i][j] if j <= i else zero for j in range(STEPS)], axis=1) for i in range(STEPS)], axis=0
    )
    inverse = jnp.concatenate(
        [jnp.concatenate([inv[i][j] if j <= i else zero for j in range(STEPS)], axis=1) for i in range(STEPS)], axis=0
    )
    return factor, inverse


def shards(kernel):
    row_count = lax.axis_size("row")
    col_count = lax.axis_size("col")
    row_index = lax.axis_index("row")
    col_index = lax.axis_index("col")
    rows_local, cols_local = kernel.shape
    width = STEPS * BLOCK
    row_ids = jnp.arange(rows_local) // BLOCK * row_count + row_index
    col_ids = jnp.arange(cols_local) // BLOCK * col_count + col_index

    blocks = gather_corner(kernel, row_index, col_index)
    band_cols = gather_columns(kernel, col_index)
    band_rows = gather_rows(kernel, row_index)

    factor, inverse = factor_corner(blocks)
    panels = lax.dot_general(
        band_cols, inverse, (((1,), (1,)), ((), ())),
        precision=lax.Precision.HIGHEST, preferred_element_type=jnp.float32,
    )
    across = lax.dot_general(
        band_rows, inverse, (((0,), (1,)), ((), ())),
        precision=lax.Precision.HIGHEST, preferred_element_type=jnp.float32,
    )
    own = lax.dynamic_slice_in_dim(factor, jnp.minimum(row_index, STEPS - 1) * BLOCK, BLOCK, 0)
    head = jnp.where(row_index < STEPS, own, panels[:BLOCK])
    panels = lax.dynamic_update_slice(panels, head, (0, 0))
    update = lax.dot_general(
        panels, across, (((1,), (1,)), ((), ())),
        precision=lax.Precision.HIGHEST, preferred_element_type=jnp.float32,
    )
    keep = (row_ids >= STEPS)[:, None] & (col_ids >= STEPS)[None, :]
    schur = jnp.where(keep, kernel - update, jnp.float32(0.0))
    return (schur, panels)


def solution(mesh):
    return jax.shard_map(
        shards,
        mesh=mesh,
        in_specs=(P("row", "col"),),
        out_specs=(P("row", "col"), P("row", None)),
        check_vma=False,
    )
```

```python
import jax
import jax.numpy as jnp
from jax import lax
from jax.sharding import PartitionSpec as P

BLOCK = 256
STEPS = 3


def pick(received, index, count, want):
    total = None
    for shift, part in enumerate(received):
        term = jnp.where((index - shift) % count == want, part, jnp.float32(0.0))
        total = term if total is None else total + term
    return total


def gather_corner(kernel, row_index, col_index):
    row_count = lax.axis_size("row")
    col_count = lax.axis_size("col")
    piece = kernel[:BLOCK, :BLOCK]
    heard = [piece]
    for shift in range(1, col_count):
        pairs = [
            (a * col_count + b, a * col_count + (b + shift) % col_count)
            for a in range(STEPS)
            for b in range(a + 1)
        ]
        heard.append(lax.ppermute(piece, ("row", "col"), pairs))
    bands = []
    for a in range(STEPS):
        band = jnp.concatenate([pick(heard, col_index, col_count, b) for b in range(a + 1)], axis=1)
        bands.append(jnp.pad(band, ((0, 0), (0, (STEPS - 1 - a) * BLOCK))))
    groups = [[0], list(range(1, STEPS))]
    blocks = [None] * STEPS
    for group in groups:
        width = (max(group) + 1) * BLOCK
        mine = None
        for a in group:
            term = jnp.where(row_index == a, bands[a][:, :width], jnp.float32(0.0))
            mine = term if mine is None else mine + term
        down = [mine]
        for shift in range(1, row_count):
            pairs = [
                (a * col_count + q, ((a + shift) % row_count) * col_count + q)
                for a in group
                for q in range(col_count)
            ]
            down.append(lax.ppermute(mine, ("row", "col"), pairs))
        for a in group:
            band = pick(down, row_index, row_count, a)
            blocks[a] = [band[:, b * BLOCK:(b + 1) * BLOCK] for b in range(a + 1)]
    return blocks


def gather_columns(kernel, col_index):
    rows = kernel.shape[0]
    mine = col_index < STEPS
    piece = jnp.where(mine, kernel[:, :BLOCK], jnp.float32(0.0))
    band = jnp.zeros((rows, STEPS * BLOCK), jnp.float32)
    band = lax.dynamic_update_slice(band, piece, (0, jnp.minimum(col_index, STEPS - 1) * BLOCK))
    return lax.psum(band, "col")


def gather_rows(kernel, row_index):
    cols = kernel.shape[1]
    mine = row_index < STEPS
    piece = jnp.where(mine, kernel[:BLOCK, :], jnp.float32(0.0))
    band = jnp.zeros((STEPS * BLOCK, cols), jnp.float32)
    band = lax.dynamic_update_slice(band, piece, (jnp.minimum(row_index, STEPS - 1) * BLOCK, 0))
    return lax.psum(band, "row")


def mul(a, b, transpose_b=False):
    dims = (((1,), (1 if transpose_b else 0,)), ((), ()))
    return lax.dot_general(a, b, dims, precision=lax.Precision.HIGHEST, preferred_element_type=jnp.float32)


def factor_block(schur):
    half = schur.shape[0] // 2
    eye = jnp.eye(half, dtype=jnp.float32)
    top = jnp.linalg.cholesky(schur[:half, :half])
    top_inv = jax.scipy.linalg.solve_triangular(top, eye, lower=True)
    side = mul(schur[half:, :half], top_inv, True)
    bottom = jnp.linalg.cholesky(schur[half:, half:] - mul(side, side, True))
    bottom_inv = jax.scipy.linalg.solve_triangular(bottom, eye, lower=True)
    corner = -mul(bottom_inv, mul(side, top_inv))
    zero = jnp.zeros((half, half), jnp.float32)
    factor = jnp.concatenate(
        [jnp.concatenate([top, zero], axis=1), jnp.concatenate([side, bottom], axis=1)], axis=0
    )
    inverse = jnp.concatenate(
        [jnp.concatenate([top_inv, zero], axis=1), jnp.concatenate([corner, bottom_inv], axis=1)], axis=0
    )
    return factor, inverse


def factor_corner(blocks):
    zero = jnp.zeros((BLOCK, BLOCK), jnp.float32)
    lower = [[None] * STEPS for _ in range(STEPS)]
    diag_inv = []
    for k in range(STEPS):
        schur = blocks[k][k]
        for j in range(k):
            schur = schur - mul(lower[k][j], lower[k][j], True)
        lower[k][k], inverse = factor_block(schur)
        diag_inv.append(inverse)
        for i in range(k + 1, STEPS):
            below = blocks[i][k]
            for j in range(k):
                below = below - mul(lower[i][j], lower[k][j], True)
            lower[i][k] = mul(below, diag_inv[k], True)
    inv = [[None] * STEPS for _ in range(STEPS)]
    for i in range(STEPS):
        inv[i][i] = diag_inv[i]
        for j in range(i - 1, -1, -1):
            acc = mul(lower[i][j], inv[j][j])
            for m in range(j + 1, i):
                acc = acc + mul(lower[i][m], inv[m][j])
            inv[i][j] = -mul(diag_inv[i], acc)
    factor = jnp.concatenate(
        [jnp.concatenate([lower[i][j] if j <= i else zero for j in range(STEPS)], axis=1) for i in range(STEPS)], axis=0
    )
    inverse = jnp.concatenate(
        [jnp.concatenate([inv[i][j] if j <= i else zero for j in range(STEPS)], axis=1) for i in range(STEPS)], axis=0
    )
    return factor, inverse


def shards(kernel):
    row_count = lax.axis_size("row")
    col_count = lax.axis_size("col")
    row_index = lax.axis_index("row")
    col_index = lax.axis_index("col")
    rows_local, cols_local = kernel.shape
    width = STEPS * BLOCK
    row_ids = jnp.arange(rows_local) // BLOCK * row_count + row_index
    col_ids = jnp.arange(cols_local) // BLOCK * col_count + col_index

    blocks = gather_corner(kernel, row_index, col_index)
    band_cols = gather_columns(kernel, col_index)
    band_rows = gather_rows(kernel, row_index)

    factor, inverse = factor_corner(blocks)
    panels = lax.dot_general(
        band_cols, inverse, (((1,), (1,)), ((), ())),
        precision=lax.Precision.HIGHEST, preferred_element_type=jnp.float32,
    )
    across = lax.dot_general(
        band_rows, inverse, (((0,), (1,)), ((), ())),
        precision=lax.Precision.HIGHEST, preferred_element_type=jnp.float32,
    )
    own = lax.dynamic_slice_in_dim(factor, jnp.minimum(row_index, STEPS - 1) * BLOCK, BLOCK, 0)
    head = jnp.where(row_index < STEPS, own, panels[:BLOCK])
    panels = lax.dynamic_update_slice(panels, head, (0, 0))
    update = lax.dot_general(
        panels, across, (((1,), (1,)), ((), ())),
        precision=lax.Precision.HIGHEST, preferred_element_type=jnp.float32,
    )
    keep = (row_ids >= STEPS)[:, None] & (col_ids >= STEPS)[None, :]
    schur = jnp.where(keep, kernel - update, jnp.float32(0.0))
    return (schur, panels)


def solution(mesh):
    return jax.shard_map(
        shards,
        mesh=mesh,
        in_specs=(P("row", "col"),),
        out_specs=(P("row", "col"), P("row", None)),
        check_vma=False,
    )
```

```python
import jax
import jax.numpy as jnp
from jax import lax
from jax.sharding import PartitionSpec as P

BLOCK = 256
STEPS = 3


def pick(received, index, count, want):
    total = None
    for shift, part in enumerate(received):
        term = jnp.where((index - shift) % count == want, part, jnp.float32(0.0))
        total = term if total is None else total + term
    return total


def gather_corner(kernel, row_index, col_index):
    row_count = lax.axis_size("row")
    col_count = lax.axis_size("col")
    piece = kernel[:BLOCK, :BLOCK]
    heard = [piece]
    for shift in range(1, col_count):
        pairs = [
            (a * col_count + b, a * col_count + (b + shift) % col_count)
            for a in range(STEPS)
            for b in range(a + 1)
        ]
        heard.append(lax.ppermute(piece, ("row", "col"), pairs))
    bands = []
    for a in range(STEPS):
        band = jnp.concatenate([pick(heard, col_index, col_count, b) for b in range(a + 1)], axis=1)
        bands.append(jnp.pad(band, ((0, 0), (0, (STEPS - 1 - a) * BLOCK))))
    groups = [[0], list(range(1, STEPS))]
    blocks = [None] * STEPS
    for group in groups:
        width = (max(group) + 1) * BLOCK
        mine = None
        for a in group:
            term = jnp.where(row_index == a, bands[a][:, :width], jnp.float32(0.0))
            mine = term if mine is None else mine + term
        down = [mine]
        for shift in range(1, row_count):
            pairs = [
                (a * col_count + q, ((a + shift) % row_count) * col_count + q)
                for a in group
                for q in range(col_count)
            ]
            down.append(lax.ppermute(mine, ("row", "col"), pairs))
        for a in group:
            band = pick(down, row_index, row_count, a)
            blocks[a] = [band[:, b * BLOCK:(b + 1) * BLOCK] for b in range(a + 1)]
    return blocks


def gather_columns(kernel, col_index):
    rows = kernel.shape[0]
    mine = col_index < STEPS
    piece = jnp.where(mine, kernel[:, :BLOCK], jnp.float32(0.0))
    band = jnp.zeros((rows, STEPS * BLOCK), jnp.float32)
    band = lax.dynamic_update_slice(band, piece, (0, jnp.minimum(col_index, STEPS - 1) * BLOCK))
    return lax.psum(band, "col")


def gather_rows(kernel, row_index):
    cols = kernel.shape[1]
    mine = row_index < STEPS
    piece = jnp.where(mine, kernel[:BLOCK, :], jnp.float32(0.0))
    band = jnp.zeros((STEPS * BLOCK, cols), jnp.float32)
    band = lax.dynamic_update_slice(band, piece, (jnp.minimum(row_index, STEPS - 1) * BLOCK, 0))
    return lax.psum(band, "row")


def mul(a, b, transpose_b=False):
    dims = (((1,), (1 if transpose_b else 0,)), ((), ()))
    return lax.dot_general(a, b, dims, precision=lax.Precision.HIGHEST, preferred_element_type=jnp.float32)


def factor_block(schur):
    half = schur.shape[0] // 2
    eye = jnp.eye(half, dtype=jnp.float32)
    top = jnp.linalg.cholesky(schur[:half, :half])
    top_inv = jax.scipy.linalg.solve_triangular(top, eye, lower=True)
    side = mul(schur[half:, :half], top_inv, True)
    bottom = jnp.linalg.cholesky(schur[half:, half:] - mul(side, side, True))
    bottom_inv = jax.scipy.linalg.solve_triangular(bottom, eye, lower=True)
    corner = -mul(bottom_inv, mul(side, top_inv))
    zero = jnp.zeros((half, half), jnp.float32)
    factor = jnp.concatenate(
        [jnp.concatenate([top, zero], axis=1), jnp.concatenate([side, bottom], axis=1)], axis=0
    )
    inverse = jnp.concatenate(
        [jnp.concatenate([top_inv, zero], axis=1), jnp.concatenate([corner, bottom_inv], axis=1)], axis=0
    )
    return factor, inverse


def factor_corner(blocks):
    zero = jnp.zeros((BLOCK, BLOCK), jnp.float32)
    lower = [[None] * STEPS for _ in range(STEPS)]
    diag_inv = []
    for k in range(STEPS):
        schur = blocks[k][k]
        for j in range(k):
            schur = schur - mul(lower[k][j], lower[k][j], True)
        lower[k][k], inverse = factor_block(schur)
        diag_inv.append(inverse)
        for i in range(k + 1, STEPS):
            below = blocks[i][k]
            for j in range(k):
                below = below - mul(lower[i][j], lower[k][j], True)
            lower[i][k] = mul(below, diag_inv[k], True)
    inv = [[None] * STEPS for _ in range(STEPS)]
    for i in range(STEPS):
        inv[i][i] = diag_inv[i]
        for j in range(i - 1, -1, -1):
            acc = mul(lower[i][j], inv[j][j])
            for m in range(j + 1, i):
                acc = acc + mul(lower[i][m], inv[m][j])
            inv[i][j] = -mul(diag_inv[i], acc)
    factor = jnp.concatenate(
        [jnp.concatenate([lower[i][j] if j <= i else zero for j in range(STEPS)], axis=1) for i in range(STEPS)], axis=0
    )
    inverse = jnp.concatenate(
        [jnp.concatenate([inv[i][j] if j <= i else zero for j in range(STEPS)], axis=1) for i in range(STEPS)], axis=0
    )
    return factor, inverse


def apply_inverse(band, inverse, axis):
    parts = []
    for j in range(STEPS):
        hi = (j + 1) * BLOCK
        piece = lax.slice_in_dim(band, 0, hi, axis=axis)
        parts.append(lax.dot_general(
            piece, inverse[j * BLOCK:hi, :hi], (((axis,), (1,)), ((), ())),
            precision=lax.Precision.HIGHEST, preferred_element_type=jnp.float32,
        ))
    return jnp.concatenate(parts, axis=1)


def shards(kernel):
    row_count = lax.axis_size("row")
    col_count = lax.axis_size("col")
    row_index = lax.axis_index("row")
    col_index = lax.axis_index("col")
    rows_local, cols_local = kernel.shape
    width = STEPS * BLOCK
    row_ids = jnp.arange(rows_local) // BLOCK * row_count + row_index
    col_ids = jnp.arange(cols_local) // BLOCK * col_count + col_index

    blocks = gather_corner(kernel, row_index, col_index)
    band_cols = gather_columns(kernel, col_index)
    band_rows = gather_rows(kernel, row_index)

    factor, inverse = factor_corner(blocks)
    panels = apply_inverse(band_cols, inverse, 1)
    across = apply_inverse(band_rows, inverse, 0)
    own = lax.dynamic_slice_in_dim(factor, jnp.minimum(row_index, STEPS - 1) * BLOCK, BLOCK, 0)
    head = jnp.where(row_index < STEPS, own, panels[:BLOCK])
    panels = lax.dynamic_update_slice(panels, head, (0, 0))
    update = lax.dot_general(
        panels, across, (((1,), (1,)), ((), ())),
        precision=lax.Precision.HIGHEST, preferred_element_type=jnp.float32,
    )
    keep = (row_ids >= STEPS)[:, None] & (col_ids >= STEPS)[None, :]
    schur = jnp.where(keep, kernel - update, jnp.float32(0.0))
    return (schur, panels)


def solution(mesh):
    return jax.shard_map(
        shards,
        mesh=mesh,
        in_specs=(P("row", "col"),),
        out_specs=(P("row", "col"), P("row", None)),
        check_vma=False,
    )
```

```python
import jax
import jax.numpy as jnp
from jax import lax
from jax.sharding import PartitionSpec as P

BLOCK = 256
STEPS = 3


def pick(received, index, count, want):
    total = None
    for shift, part in enumerate(received):
        term = jnp.where((index - shift) % count == want, part, jnp.float32(0.0))
        total = term if total is None else total + term
    return total


def gather_corner(kernel, row_index, col_index):
    row_count = lax.axis_size("row")
    col_count = lax.axis_size("col")
    ring = 4
    rings = col_count // ring
    piece = kernel[:BLOCK, :BLOCK]
    heard = [piece]
    for shift in range(1, ring):
        pairs = [
            (a * col_count + b, a * col_count + (b + shift) % ring)
            for a in range(STEPS)
            for b in range(a + 1)
        ]
        heard.append(lax.ppermute(piece, ("row", "col"), pairs))
    bands = []
    for a in range(STEPS):
        band = jnp.concatenate([pick(heard, col_index % ring, ring, b) for b in range(a + 1)], axis=1)
        bands.append(jnp.pad(band, ((0, 0), (0, (STEPS - 1 - a) * BLOCK))))
    groups = [[0], list(range(1, STEPS))]
    blocks = [None] * STEPS
    for group in groups:
        width = (max(group) + 1) * BLOCK
        mine = None
        for a in group:
            term = jnp.where(row_index == a, bands[a][:, :width], jnp.float32(0.0))
            mine = term if mine is None else mine + term
        across = [mine]
        for hop in range(1, rings):
            pairs = [(a * col_count + z, a * col_count + hop * ring + z) for a in group for z in range(ring)]
            across.append(lax.ppermute(mine, ("row", "col"), pairs))
        mine = pick(across, col_index // ring, rings, 0)
        down = [mine]
        for shift in range(1, row_count):
            pairs = [
                (a * col_count + q, ((a + shift) % row_count) * col_count + q)
                for a in group
                for q in range(col_count)
            ]
            down.append(lax.ppermute(mine, ("row", "col"), pairs))
        for a in group:
            band = pick(down, row_index, row_count, a)
            blocks[a] = [band[:, b * BLOCK:(b + 1) * BLOCK] for b in range(a + 1)]
    return blocks


def gather_columns(kernel, col_index):
    rows = kernel.shape[0]
    mine = col_index < STEPS
    piece = jnp.where(mine, kernel[:, :BLOCK], jnp.float32(0.0))
    band = jnp.zeros((rows, STEPS * BLOCK), jnp.float32)
    band = lax.dynamic_update_slice(band, piece, (0, jnp.minimum(col_index, STEPS - 1) * BLOCK))
    return lax.psum(band, "col")


def gather_rows(kernel, row_index):
    cols = kernel.shape[1]
    mine = row_index < STEPS
    piece = jnp.where(mine, kernel[:BLOCK, :], jnp.float32(0.0))
    band = jnp.zeros((STEPS * BLOCK, cols), jnp.float32)
    band = lax.dynamic_update_slice(band, piece, (jnp.minimum(row_index, STEPS - 1) * BLOCK, 0))
    return lax.psum(band, "row")


def mul(a, b, transpose_b=False):
    dims = (((1,), (1 if transpose_b else 0,)), ((), ()))
    return lax.dot_general(a, b, dims, precision=lax.Precision.HIGHEST, preferred_element_type=jnp.float32)


def factor_block(schur):
    half = schur.shape[0] // 2
    eye = jnp.eye(half, dtype=jnp.float32)
    top = jnp.linalg.cholesky(schur[:half, :half])
    top_inv = jax.scipy.linalg.solve_triangular(top, eye, lower=True)
    side = mul(schur[half:, :half], top_inv, True)
    bottom = jnp.linalg.cholesky(schur[half:, half:] - mul(side, side, True))
    bottom_inv = jax.scipy.linalg.solve_triangular(bottom, eye, lower=True)
    corner = -mul(bottom_inv, mul(side, top_inv))
    zero = jnp.zeros((half, half), jnp.float32)
    factor = jnp.concatenate(
        [jnp.concatenate([top, zero], axis=1), jnp.concatenate([side, bottom], axis=1)], axis=0
    )
    inverse = jnp.concatenate(
        [jnp.concatenate([top_inv, zero], axis=1), jnp.concatenate([corner, bottom_inv], axis=1)], axis=0
    )
    return factor, inverse


def factor_corner(blocks):
    zero = jnp.zeros((BLOCK, BLOCK), jnp.float32)
    lower = [[None] * STEPS for _ in range(STEPS)]
    diag_inv = []
    for k in range(STEPS):
        schur = blocks[k][k]
        for j in range(k):
            schur = schur - mul(lower[k][j], lower[k][j], True)
        lower[k][k], inverse = factor_block(schur)
        diag_inv.append(inverse)
        for i in range(k + 1, STEPS):
            below = blocks[i][k]
            for j in range(k):
                below = below - mul(lower[i][j], lower[k][j], True)
            lower[i][k] = mul(below, diag_inv[k], True)
    inv = [[None] * STEPS for _ in range(STEPS)]
    for i in range(STEPS):
        inv[i][i] = diag_inv[i]
        for j in range(i - 1, -1, -1):
            acc = mul(lower[i][j], inv[j][j])
            for m in range(j + 1, i):
                acc = acc + mul(lower[i][m], inv[m][j])
            inv[i][j] = -mul(diag_inv[i], acc)
    factor = jnp.concatenate(
        [jnp.concatenate([lower[i][j] if j <= i else zero for j in range(STEPS)], axis=1) for i in range(STEPS)], axis=0
    )
    inverse = jnp.concatenate(
        [jnp.concatenate([inv[i][j] if j <= i else zero for j in range(STEPS)], axis=1) for i in range(STEPS)], axis=0
    )
    return factor, inverse


def apply_inverse(band, inverse, axis):
    parts = []
    for j in range(STEPS):
        hi = (j + 1) * BLOCK
        piece = lax.slice_in_dim(band, 0, hi, axis=axis)
        parts.append(lax.dot_general(
            piece, inverse[j * BLOCK:hi, :hi], (((axis,), (1,)), ((), ())),
            precision=lax.Precision.HIGHEST, preferred_element_type=jnp.float32,
        ))
    return jnp.concatenate(parts, axis=1)


def shards(kernel):
    row_count = lax.axis_size("row")
    col_count = lax.axis_size("col")
    row_index = lax.axis_index("row")
    col_index = lax.axis_index("col")
    rows_local, cols_local = kernel.shape
    width = STEPS * BLOCK
    row_ids = jnp.arange(rows_local) // BLOCK * row_count + row_index
    col_ids = jnp.arange(cols_local) // BLOCK * col_count + col_index

    blocks = gather_corner(kernel, row_index, col_index)
    band_cols = gather_columns(kernel, col_index)
    band_rows = gather_rows(kernel, row_index)

    factor, inverse = factor_corner(blocks)
    panels = apply_inverse(band_cols, inverse, 1)
    across = apply_inverse(band_rows, inverse, 0)
    own = lax.dynamic_slice_in_dim(factor, jnp.minimum(row_index, STEPS - 1) * BLOCK, BLOCK, 0)
    head = jnp.where(row_index < STEPS, own, panels[:BLOCK])
    panels = lax.dynamic_update_slice(panels, head, (0, 0))
    update = lax.dot_general(
        panels, across, (((1,), (1,)), ((), ())),
        precision=lax.Precision.HIGHEST, preferred_element_type=jnp.float32,
    )
    keep = (row_ids >= STEPS)[:, None] & (col_ids >= STEPS)[None, :]
    schur = jnp.where(keep, kernel - update, jnp.float32(0.0))
    return (schur, panels)


def solution(mesh):
    return jax.shard_map(
        shards,
        mesh=mesh,
        in_specs=(P("row", "col"),),
        out_specs=(P("row", "col"), P("row", None)),
        check_vma=False,
    )
```

```python
import jax
import jax.numpy as jnp
from jax import lax
from jax.sharding import PartitionSpec as P

BLOCK = 256
STEPS = 3


def pick(received, index, count, want):
    total = None
    for shift, part in enumerate(received):
        term = jnp.where((index - shift) % count == want, part, jnp.float32(0.0))
        total = term if total is None else total + term
    return total


def gather_corner(kernel, row_index, col_index):
    row_count = lax.axis_size("row")
    col_count = lax.axis_size("col")
    ring = 4
    rings = col_count // ring
    piece = kernel[:BLOCK, :BLOCK]
    heard = [piece]
    for shift in range(1, ring):
        pairs = [
            (a * col_count + b, a * col_count + (b + shift) % ring)
            for a in range(STEPS)
            for b in range(a + 1)
        ]
        heard.append(lax.ppermute(piece, ("row", "col"), pairs))
    bands = []
    for a in range(STEPS):
        band = jnp.concatenate([pick(heard, col_index % ring, ring, b) for b in range(a + 1)], axis=1)
        bands.append(jnp.pad(band, ((0, 0), (0, (STEPS - 1 - a) * BLOCK))))
    groups = [[0], list(range(1, STEPS))]
    blocks = [None] * STEPS
    for group in groups:
        width = (max(group) + 1) * BLOCK
        mine = None
        for a in group:
            term = jnp.where(row_index == a, bands[a][:, :width], jnp.float32(0.0))
            mine = term if mine is None else mine + term
        across = [mine]
        for hop in range(1, rings):
            pairs = [(a * col_count + z, a * col_count + hop * ring + z) for a in group for z in range(ring)]
            across.append(lax.ppermute(mine, ("row", "col"), pairs))
        mine = pick(across, col_index // ring, rings, 0)
        if len(group) == 1:
            down = [mine]
            for shift in range(1, row_count):
                pairs = [
                    (a * col_count + q, ((a + shift) % row_count) * col_count + q)
                    for a in group
                    for q in range(col_count)
                ]
                down.append(lax.ppermute(mine, ("row", "col"), pairs))
            for a in group:
                band = pick(down, row_index, row_count, a)
                blocks[a] = [band[:, b * BLOCK:(b + 1) * BLOCK] for b in range(a + 1)]
            continue
        odd = row_index % 2 == 1
        held = mine
        for shift in range(1, row_count // 2):
            pairs = [
                (a * col_count + q, ((a + 2 * shift) % row_count) * col_count + q)
                for a in group
                for q in range(col_count)
            ]
            got = lax.ppermute(mine, ("row", "col"), pairs)
            source = 2 - row_index % 2
            held = held + jnp.where((row_index - 2 * shift) % row_count == source, got, jnp.float32(0.0))
        pairs = [(p * col_count + q, (p ^ 1) * col_count + q) for p in range(row_count) for q in range(col_count)]
        other = lax.ppermute(held, ("row", "col"), pairs)
        for a in group:
            band = jnp.where(odd == (a % 2 == 1), held, other)
            blocks[a] = [band[:, b * BLOCK:(b + 1) * BLOCK] for b in range(a + 1)]
    return blocks


def gather_columns(kernel, col_index):
    rows = kernel.shape[0]
    mine = col_index < STEPS
    piece = jnp.where(mine, kernel[:, :BLOCK], jnp.float32(0.0))
    band = jnp.zeros((rows, STEPS * BLOCK), jnp.float32)
    band = lax.dynamic_update_slice(band, piece, (0, jnp.minimum(col_index, STEPS - 1) * BLOCK))
    return lax.psum(band, "col")


def gather_rows(kernel, row_index):
    cols = kernel.shape[1]
    mine = row_index < STEPS
    piece = jnp.where(mine, kernel[:BLOCK, :], jnp.float32(0.0))
    band = jnp.zeros((STEPS * BLOCK, cols), jnp.float32)
    band = lax.dynamic_update_slice(band, piece, (jnp.minimum(row_index, STEPS - 1) * BLOCK, 0))
    return lax.psum(band, "row")


def mul(a, b, transpose_b=False):
    dims = (((1,), (1 if transpose_b else 0,)), ((), ()))
    return lax.dot_general(a, b, dims, precision=lax.Precision.HIGHEST, preferred_element_type=jnp.float32)


def factor_block(schur):
    half = schur.shape[0] // 2
    eye = jnp.eye(half, dtype=jnp.float32)
    top = jnp.linalg.cholesky(schur[:half, :half])
    top_inv = jax.scipy.linalg.solve_triangular(top, eye, lower=True)
    side = mul(schur[half:, :half], top_inv, True)
    bottom = jnp.linalg.cholesky(schur[half:, half:] - mul(side, side, True))
    bottom_inv = jax.scipy.linalg.solve_triangular(bottom, eye, lower=True)
    corner = -mul(bottom_inv, mul(side, top_inv))
    zero = jnp.zeros((half, half), jnp.float32)
    factor = jnp.concatenate(
        [jnp.concatenate([top, zero], axis=1), jnp.concatenate([side, bottom], axis=1)], axis=0
    )
    inverse = jnp.concatenate(
        [jnp.concatenate([top_inv, zero], axis=1), jnp.concatenate([corner, bottom_inv], axis=1)], axis=0
    )
    return factor, inverse


def factor_corner(blocks):
    zero = jnp.zeros((BLOCK, BLOCK), jnp.float32)
    lower = [[None] * STEPS for _ in range(STEPS)]
    diag_inv = []
    for k in range(STEPS):
        schur = blocks[k][k]
        for j in range(k):
            schur = schur - mul(lower[k][j], lower[k][j], True)
        lower[k][k], inverse = factor_block(schur)
        diag_inv.append(inverse)
        for i in range(k + 1, STEPS):
            below = blocks[i][k]
            for j in range(k):
                below = below - mul(lower[i][j], lower[k][j], True)
            lower[i][k] = mul(below, diag_inv[k], True)
    inv = [[None] * STEPS for _ in range(STEPS)]
    for i in range(STEPS):
        inv[i][i] = diag_inv[i]
        for j in range(i - 1, -1, -1):
            acc = mul(lower[i][j], inv[j][j])
            for m in range(j + 1, i):
                acc = acc + mul(lower[i][m], inv[m][j])
            inv[i][j] = -mul(diag_inv[i], acc)
    factor = jnp.concatenate(
        [jnp.concatenate([lower[i][j] if j <= i else zero for j in range(STEPS)], axis=1) for i in range(STEPS)], axis=0
    )
    inverse = jnp.concatenate(
        [jnp.concatenate([inv[i][j] if j <= i else zero for j in range(STEPS)], axis=1) for i in range(STEPS)], axis=0
    )
    return factor, inverse


def apply_inverse(band, inverse, axis):
    parts = []
    for j in range(STEPS):
        hi = (j + 1) * BLOCK
        piece = lax.slice_in_dim(band, 0, hi, axis=axis)
        parts.append(lax.dot_general(
            piece, inverse[j * BLOCK:hi, :hi], (((axis,), (1,)), ((), ())),
            precision=lax.Precision.HIGHEST, preferred_element_type=jnp.float32,
        ))
    return jnp.concatenate(parts, axis=1)


def shards(kernel):
    row_count = lax.axis_size("row")
    col_count = lax.axis_size("col")
    row_index = lax.axis_index("row")
    col_index = lax.axis_index("col")
    rows_local, cols_local = kernel.shape
    width = STEPS * BLOCK
    row_ids = jnp.arange(rows_local) // BLOCK * row_count + row_index
    col_ids = jnp.arange(cols_local) // BLOCK * col_count + col_index

    blocks = gather_corner(kernel, row_index, col_index)
    band_cols = gather_columns(kernel, col_index)
    band_rows = gather_rows(kernel, row_index)

    factor, inverse = factor_corner(blocks)
    panels = apply_inverse(band_cols, inverse, 1)
    across = apply_inverse(band_rows, inverse, 0)
    own = lax.dynamic_slice_in_dim(factor, jnp.minimum(row_index, STEPS - 1) * BLOCK, BLOCK, 0)
    head = jnp.where(row_index < STEPS, own, panels[:BLOCK])
    panels = lax.dynamic_update_slice(panels, head, (0, 0))
    update = lax.dot_general(
        panels, across, (((1,), (1,)), ((), ())),
        precision=lax.Precision.HIGHEST, preferred_element_type=jnp.float32,
    )
    keep = (row_ids >= STEPS)[:, None] & (col_ids >= STEPS)[None, :]
    schur = jnp.where(keep, kernel - update, jnp.float32(0.0))
    return (schur, panels)


def solution(mesh):
    return jax.shard_map(
        shards,
        mesh=mesh,
        in_specs=(P("row", "col"),),
        out_specs=(P("row", "col"), P("row", None)),
        check_vma=False,
    )
```

```python
import jax
import jax.numpy as jnp
from jax import lax
from jax.sharding import PartitionSpec as P

BLOCK = 256
STEPS = 3


def pick(received, index, count, want):
    total = None
    for shift, part in enumerate(received):
        term = jnp.where((index - shift) % count == want, part, jnp.float32(0.0))
        total = term if total is None else total + term
    return total


def gather_corner(kernel, row_index, col_index):
    row_count = lax.axis_size("row")
    col_count = lax.axis_size("col")
    ring = 4
    rings = col_count // ring
    piece = kernel[:BLOCK, :BLOCK]
    heard = [piece]
    for shift in range(1, ring):
        pairs = [
            (a * col_count + b, a * col_count + (b + shift) % ring)
            for a in range(STEPS)
            for b in range(a + 1)
        ]
        heard.append(lax.ppermute(piece, ("row", "col"), pairs))
    bands = []
    for a in range(STEPS):
        band = jnp.concatenate([pick(heard, col_index % ring, ring, b) for b in range(a + 1)], axis=1)
        bands.append(jnp.pad(band, ((0, 0), (0, (STEPS - 1 - a) * BLOCK))))
    groups = [[0], list(range(1, STEPS))]
    blocks = [None] * STEPS
    for group in groups:
        width = (max(group) + 1) * BLOCK
        mine = None
        for a in group:
            term = jnp.where(row_index == a, bands[a][:, :width], jnp.float32(0.0))
            mine = term if mine is None else mine + term
        across = [mine]
        for hop in range(1, rings):
            pairs = [(a * col_count + z, a * col_count + hop * ring + z) for a in group for z in range(ring)]
            across.append(lax.ppermute(mine, ("row", "col"), pairs))
        mine = pick(across, col_index // ring, rings, 0)
        odd = row_index % 2 == 1
        held = mine
        for shift in range(1, row_count // 2):
            pairs = [
                (a * col_count + q, ((a + 2 * shift) % row_count) * col_count + q)
                for a in group
                for q in range(col_count)
            ]
            got = lax.ppermute(mine, ("row", "col"), pairs)
            source = 0 if len(group) == 1 else 2 - row_index % 2
            held = held + jnp.where((row_index - 2 * shift) % row_count == source, got, jnp.float32(0.0))
        pairs = [(p * col_count + q, (p ^ 1) * col_count + q) for p in range(row_count) for q in range(col_count)]
        other = lax.ppermute(held, ("row", "col"), pairs)
        for a in group:
            band = jnp.where(odd == (a % 2 == 1), held, other)
            blocks[a] = [band[:, b * BLOCK:(b + 1) * BLOCK] for b in range(a + 1)]
    return blocks


def gather_columns(kernel, col_index):
    rows = kernel.shape[0]
    mine = col_index < STEPS
    piece = jnp.where(mine, kernel[:, :BLOCK], jnp.float32(0.0))
    band = jnp.zeros((rows, STEPS * BLOCK), jnp.float32)
    band = lax.dynamic_update_slice(band, piece, (0, jnp.minimum(col_index, STEPS - 1) * BLOCK))
    return lax.psum(band, "col")


def gather_rows(kernel, row_index):
    cols = kernel.shape[1]
    mine = row_index < STEPS
    piece = jnp.where(mine, kernel[:BLOCK, :], jnp.float32(0.0))
    band = jnp.zeros((STEPS * BLOCK, cols), jnp.float32)
    band = lax.dynamic_update_slice(band, piece, (jnp.minimum(row_index, STEPS - 1) * BLOCK, 0))
    return lax.psum(band, "row")


def mul(a, b, transpose_b=False):
    dims = (((1,), (1 if transpose_b else 0,)), ((), ()))
    return lax.dot_general(a, b, dims, precision=lax.Precision.HIGHEST, preferred_element_type=jnp.float32)


def factor_block(schur):
    half = schur.shape[0] // 2
    eye = jnp.eye(half, dtype=jnp.float32)
    top = jnp.linalg.cholesky(schur[:half, :half])
    top_inv = jax.scipy.linalg.solve_triangular(top, eye, lower=True)
    side = mul(schur[half:, :half], top_inv, True)
    bottom = jnp.linalg.cholesky(schur[half:, half:] - mul(side, side, True))
    bottom_inv = jax.scipy.linalg.solve_triangular(bottom, eye, lower=True)
    corner = -mul(bottom_inv, mul(side, top_inv))
    zero = jnp.zeros((half, half), jnp.float32)
    factor = jnp.concatenate(
        [jnp.concatenate([top, zero], axis=1), jnp.concatenate([side, bottom], axis=1)], axis=0
    )
    inverse = jnp.concatenate(
        [jnp.concatenate([top_inv, zero], axis=1), jnp.concatenate([corner, bottom_inv], axis=1)], axis=0
    )
    return factor, inverse


def factor_corner(blocks):
    zero = jnp.zeros((BLOCK, BLOCK), jnp.float32)
    lower = [[None] * STEPS for _ in range(STEPS)]
    diag_inv = []
    for k in range(STEPS):
        schur = blocks[k][k]
        for j in range(k):
            schur = schur - mul(lower[k][j], lower[k][j], True)
        lower[k][k], inverse = factor_block(schur)
        diag_inv.append(inverse)
        for i in range(k + 1, STEPS):
            below = blocks[i][k]
            for j in range(k):
                below = below - mul(lower[i][j], lower[k][j], True)
            lower[i][k] = mul(below, diag_inv[k], True)
    inv = [[None] * STEPS for _ in range(STEPS)]
    for i in range(STEPS):
        inv[i][i] = diag_inv[i]
        for j in range(i - 1, -1, -1):
            acc = mul(lower[i][j], inv[j][j])
            for m in range(j + 1, i):
                acc = acc + mul(lower[i][m], inv[m][j])
            inv[i][j] = -mul(diag_inv[i], acc)
    factor = jnp.concatenate(
        [jnp.concatenate([lower[i][j] if j <= i else zero for j in range(STEPS)], axis=1) for i in range(STEPS)], axis=0
    )
    inverse = jnp.concatenate(
        [jnp.concatenate([inv[i][j] if j <= i else zero for j in range(STEPS)], axis=1) for i in range(STEPS)], axis=0
    )
    return factor, inverse


def apply_inverse(band, inverse, axis):
    parts = []
    for j in range(STEPS):
        hi = (j + 1) * BLOCK
        piece = lax.slice_in_dim(band, 0, hi, axis=axis)
        parts.append(lax.dot_general(
            piece, inverse[j * BLOCK:hi, :hi], (((axis,), (1,)), ((), ())),
            precision=lax.Precision.HIGHEST, preferred_element_type=jnp.float32,
        ))
    return jnp.concatenate(parts, axis=1)


def shards(kernel):
    row_count = lax.axis_size("row")
    col_count = lax.axis_size("col")
    row_index = lax.axis_index("row")
    col_index = lax.axis_index("col")
    rows_local, cols_local = kernel.shape
    width = STEPS * BLOCK
    row_ids = jnp.arange(rows_local) // BLOCK * row_count + row_index
    col_ids = jnp.arange(cols_local) // BLOCK * col_count + col_index

    blocks = gather_corner(kernel, row_index, col_index)
    band_cols = gather_columns(kernel, col_index)
    band_rows = gather_rows(kernel, row_index)

    factor, inverse = factor_corner(blocks)
    panels = apply_inverse(band_cols, inverse, 1)
    across = apply_inverse(band_rows, inverse, 0)
    own = lax.dynamic_slice_in_dim(factor, jnp.minimum(row_index, STEPS - 1) * BLOCK, BLOCK, 0)
    head = jnp.where(row_index < STEPS, own, panels[:BLOCK])
    panels = lax.dynamic_update_slice(panels, head, (0, 0))
    update = lax.dot_general(
        panels, across, (((1,), (1,)), ((), ())),
        precision=lax.Precision.HIGHEST, preferred_element_type=jnp.float32,
    )
    keep = (row_ids >= STEPS)[:, None] & (col_ids >= STEPS)[None, :]
    schur = jnp.where(keep, kernel - update, jnp.float32(0.0))
    return (schur, panels)


def solution(mesh):
    return jax.shard_map(
        shards,
        mesh=mesh,
        in_specs=(P("row", "col"),),
        out_specs=(P("row", "col"), P("row", None)),
        check_vma=False,
    )
```

```python
import jax
import jax.numpy as jnp
from jax import lax
from jax.sharding import PartitionSpec as P

BLOCK = 256
STEPS = 3


def pick(received, index, count, want):
    total = None
    for shift, part in enumerate(received):
        term = jnp.where((index - shift) % count == want, part, jnp.float32(0.0))
        total = term if total is None else total + term
    return total


def gather_corner(kernel, row_index, col_index):
    row_count = lax.axis_size("row")
    col_count = lax.axis_size("col")
    ring = 4
    rings = col_count // ring
    piece = kernel[:BLOCK, :BLOCK]
    heard = [piece]
    for shift in range(1, ring):
        pairs = [
            (a * col_count + b, a * col_count + (b + shift) % ring)
            for a in range(STEPS)
            for b in range(a + 1)
        ]
        heard.append(lax.ppermute(piece, ("row", "col"), pairs))
    bands = []
    for a in range(STEPS):
        band = jnp.concatenate([pick(heard, col_index % ring, ring, b) for b in range(a + 1)], axis=1)
        bands.append(jnp.pad(band, ((0, 0), (0, (STEPS - 1 - a) * BLOCK))))
    groups = [[0], list(range(1, STEPS))]
    blocks = [None] * STEPS
    for group in groups:
        width = (max(group) + 1) * BLOCK
        mine = None
        for a in group:
            term = jnp.where(row_index == a, bands[a][:, :width], jnp.float32(0.0))
            mine = term if mine is None else mine + term
        across = [mine]
        for hop in range(1, rings):
            pairs = [(a * col_count + z, a * col_count + hop * ring + z) for a in group for z in range(ring)]
            across.append(lax.ppermute(mine, ("row", "col"), pairs))
        mine = pick(across, col_index // ring, rings, 0)
        odd = row_index % 2 == 1
        held = mine
        for shift in range(1, row_count // 2):
            pairs = [
                (a * col_count + q, ((a + 2 * shift) % row_count) * col_count + q)
                for a in group
                for q in range(col_count)
            ]
            got = lax.ppermute(mine, ("row", "col"), pairs)
            source = 0 if len(group) == 1 else 2 - row_index % 2
            held = held + jnp.where((row_index - 2 * shift) % row_count == source, got, jnp.float32(0.0))
        pairs = [(p * col_count + q, (p ^ 1) * col_count + q) for p in range(row_count) for q in range(col_count)]
        other = lax.ppermute(held, ("row", "col"), pairs)
        for a in group:
            band = jnp.where(odd == (a % 2 == 1), held, other)
            blocks[a] = [band[:, b * BLOCK:(b + 1) * BLOCK] for b in range(a + 1)]
    return blocks


def gather_columns(kernel, col_index):
    rows = kernel.shape[0]
    mine = col_index < STEPS
    piece = jnp.where(mine, kernel[:, :BLOCK], jnp.float32(0.0))
    band = jnp.zeros((rows, STEPS * BLOCK), jnp.float32)
    band = lax.dynamic_update_slice(band, piece, (0, jnp.minimum(col_index, STEPS - 1) * BLOCK))
    return lax.psum(band, "col")


def gather_rows(kernel, row_index):
    cols = kernel.shape[1]
    mine = row_index < STEPS
    piece = jnp.where(mine, kernel[:BLOCK, :], jnp.float32(0.0))
    band = jnp.zeros((STEPS * BLOCK, cols), jnp.float32)
    band = lax.dynamic_update_slice(band, piece, (jnp.minimum(row_index, STEPS - 1) * BLOCK, 0))
    return lax.psum(band, "row")


def mul(a, b, transpose_b=False):
    dims = (((1,), (1 if transpose_b else 0,)), ((), ()))
    return lax.dot_general(a, b, dims, precision=lax.Precision.HIGHEST, preferred_element_type=jnp.float32)


def factor_block(schur):
    half = schur.shape[0] // 2
    eye = jnp.eye(half, dtype=jnp.float32)
    top = jnp.linalg.cholesky(schur[:half, :half])
    top_inv = jax.scipy.linalg.solve_triangular(top, eye, lower=True)
    side = mul(schur[half:, :half], top_inv, True)
    bottom = jnp.linalg.cholesky(schur[half:, half:] - mul(side, side, True))
    bottom_inv = jax.scipy.linalg.solve_triangular(bottom, eye, lower=True)
    corner = -mul(bottom_inv, mul(side, top_inv))
    zero = jnp.zeros((half, half), jnp.float32)
    factor = jnp.concatenate(
        [jnp.concatenate([top, zero], axis=1), jnp.concatenate([side, bottom], axis=1)], axis=0
    )
    inverse = jnp.concatenate(
        [jnp.concatenate([top_inv, zero], axis=1), jnp.concatenate([corner, bottom_inv], axis=1)], axis=0
    )
    return factor, inverse


def factor_corner(blocks):
    zero = jnp.zeros((BLOCK, BLOCK), jnp.float32)
    lower = [[None] * STEPS for _ in range(STEPS)]
    diag_inv = []
    for k in range(STEPS):
        schur = blocks[k][k]
        for j in range(k):
            schur = schur - mul(lower[k][j], lower[k][j], True)
        lower[k][k], inverse = factor_block(schur)
        diag_inv.append(inverse)
        for i in range(k + 1, STEPS):
            below = blocks[i][k]
            for j in range(k):
                below = below - mul(lower[i][j], lower[k][j], True)
            lower[i][k] = mul(below, diag_inv[k], True)
    inv = [[None] * STEPS for _ in range(STEPS)]
    for i in range(STEPS):
        inv[i][i] = diag_inv[i]
        for j in range(i - 1, -1, -1):
            acc = mul(lower[i][j], inv[j][j])
            for m in range(j + 1, i):
                acc = acc + mul(lower[i][m], inv[m][j])
            inv[i][j] = -mul(diag_inv[i], acc)
    factor = jnp.concatenate(
        [jnp.concatenate([lower[i][j] if j <= i else zero for j in range(STEPS)], axis=1) for i in range(STEPS)], axis=0
    )
    inverse = jnp.concatenate(
        [jnp.concatenate([inv[i][j] if j <= i else zero for j in range(STEPS)], axis=1) for i in range(STEPS)], axis=0
    )
    return factor, inverse


def apply_inverse(band, inverse, axis):
    parts = []
    for j in range(STEPS):
        hi = (j + 1) * BLOCK
        piece = lax.slice_in_dim(band, 0, hi, axis=axis)
        parts.append(lax.dot_general(
            piece, inverse[j * BLOCK:hi, :hi], (((axis,), (1,)), ((), ())),
            precision=lax.Precision.HIGHEST, preferred_element_type=jnp.float32,
        ))
    return jnp.concatenate(parts, axis=1)


def shards(kernel):
    row_count = lax.axis_size("row")
    col_count = lax.axis_size("col")
    row_index = lax.axis_index("row")
    col_index = lax.axis_index("col")
    rows_local, cols_local = kernel.shape
    width = STEPS * BLOCK
    row_ids = jnp.arange(rows_local) // BLOCK * row_count + row_index
    col_ids = jnp.arange(cols_local) // BLOCK * col_count + col_index

    blocks = gather_corner(kernel, row_index, col_index)
    band_cols = gather_columns(kernel, col_index)
    band_rows = gather_rows(kernel, row_index)

    factor, inverse = factor_corner(blocks)
    panels = apply_inverse(band_cols, inverse, 1)
    across = apply_inverse(band_rows, inverse, 0)
    own = lax.dynamic_slice_in_dim(factor, jnp.minimum(row_index, STEPS - 1) * BLOCK, BLOCK, 0)
    own = jnp.pad(own, ((0, rows_local - BLOCK), (0, 0)))
    head = (jnp.arange(rows_local) < BLOCK)[:, None] & (row_index < STEPS)
    panels = jnp.where(head, own, panels)
    update = lax.dot_general(
        panels, across, (((1,), (1,)), ((), ())),
        precision=lax.Precision.HIGHEST, preferred_element_type=jnp.float32,
    )
    keep = (row_ids >= STEPS)[:, None] & (col_ids >= STEPS)[None, :]
    schur = jnp.where(keep, kernel - update, jnp.float32(0.0))
    return (schur, panels)


def solution(mesh):
    return jax.shard_map(
        shards,
        mesh=mesh,
        in_specs=(P("row", "col"),),
        out_specs=(P("row", "col"), P("row", None)),
        check_vma=False,
    )
```

```python
import jax
import jax.numpy as jnp
from jax import lax
from jax.sharding import PartitionSpec as P

BLOCK = 256
STEPS = 3


def pick(received, index, count, want):
    total = None
    for shift, part in enumerate(received):
        term = jnp.where((index - shift) % count == want, part, jnp.float32(0.0))
        total = term if total is None else total + term
    return total


def gather_corner(kernel, row_index, col_index):
    row_count = lax.axis_size("row")
    col_count = lax.axis_size("col")
    ring = 4
    rings = col_count // ring
    piece = kernel[:BLOCK, :BLOCK]
    heard = [piece]
    for shift in range(1, ring):
        pairs = [
            (a * col_count + b, a * col_count + (b + shift) % ring)
            for a in range(STEPS)
            for b in range(a + 1)
        ]
        heard.append(lax.ppermute(piece, ("row", "col"), pairs))
    bands = []
    for a in range(STEPS):
        band = jnp.concatenate([pick(heard, col_index % ring, ring, b) for b in range(a + 1)], axis=1)
        bands.append(jnp.pad(band, ((0, 0), (0, (STEPS - 1 - a) * BLOCK))))
    groups = [[0], list(range(1, STEPS))]
    blocks = [None] * STEPS
    for group in groups:
        width = (max(group) + 1) * BLOCK
        mine = None
        for a in group:
            term = jnp.where(row_index == a, bands[a][:, :width], jnp.float32(0.0))
            mine = term if mine is None else mine + term
        across = [mine]
        for hop in range(1, rings):
            pairs = [(a * col_count + z, a * col_count + hop * ring + z) for a in group for z in range(ring)]
            across.append(lax.ppermute(mine, ("row", "col"), pairs))
        mine = pick(across, col_index // ring, rings, 0)
        odd = row_index % 2 == 1
        held = mine
        for shift in range(1, row_count // 2):
            pairs = [
                (a * col_count + q, ((a + 2 * shift) % row_count) * col_count + q)
                for a in group
                for q in range(col_count)
            ]
            got = lax.ppermute(mine, ("row", "col"), pairs)
            source = 0 if len(group) == 1 else 2 - row_index % 2
            held = held + jnp.where((row_index - 2 * shift) % row_count == source, got, jnp.float32(0.0))
        senders = range(0, row_count, 2) if len(group) == 1 else range(row_count)
        pairs = [(p * col_count + q, (p ^ 1) * col_count + q) for p in senders for q in range(col_count)]
        other = lax.ppermute(held, ("row", "col"), pairs)
        for a in group:
            band = jnp.where(odd == (a % 2 == 1), held, other)
            blocks[a] = [band[:, b * BLOCK:(b + 1) * BLOCK] for b in range(a + 1)]
    return blocks


def gather_columns(kernel, col_index):
    rows = kernel.shape[0]
    mine = col_index < STEPS
    piece = jnp.where(mine, kernel[:, :BLOCK], jnp.float32(0.0))
    band = jnp.zeros((rows, STEPS * BLOCK), jnp.float32)
    band = lax.dynamic_update_slice(band, piece, (0, jnp.minimum(col_index, STEPS - 1) * BLOCK))
    return lax.psum(band, "col")


def gather_rows(kernel, row_index):
    cols = kernel.shape[1]
    mine = row_index < STEPS
    piece = jnp.where(mine, kernel[:BLOCK, :], jnp.float32(0.0))
    band = jnp.zeros((STEPS * BLOCK, cols), jnp.float32)
    band = lax.dynamic_update_slice(band, piece, (jnp.minimum(row_index, STEPS - 1) * BLOCK, 0))
    return lax.psum(band, "row")


def mul(a, b, transpose_b=False):
    dims = (((1,), (1 if transpose_b else 0,)), ((), ()))
    return lax.dot_general(a, b, dims, precision=lax.Precision.HIGHEST, preferred_element_type=jnp.float32)


def factor_block(schur):
    half = schur.shape[0] // 2
    eye = jnp.eye(half, dtype=jnp.float32)
    top = jnp.linalg.cholesky(schur[:half, :half])
    top_inv = jax.scipy.linalg.solve_triangular(top, eye, lower=True)
    side = mul(schur[half:, :half], top_inv, True)
    bottom = jnp.linalg.cholesky(schur[half:, half:] - mul(side, side, True))
    bottom_inv = jax.scipy.linalg.solve_triangular(bottom, eye, lower=True)
    corner = -mul(bottom_inv, mul(side, top_inv))
    zero = jnp.zeros((half, half), jnp.float32)
    factor = jnp.concatenate(
        [jnp.concatenate([top, zero], axis=1), jnp.concatenate([side, bottom], axis=1)], axis=0
    )
    inverse = jnp.concatenate(
        [jnp.concatenate([top_inv, zero], axis=1), jnp.concatenate([corner, bottom_inv], axis=1)], axis=0
    )
    return factor, inverse


def factor_corner(blocks):
    zero = jnp.zeros((BLOCK, BLOCK), jnp.float32)
    lower = [[None] * STEPS for _ in range(STEPS)]
    diag_inv = []
    for k in range(STEPS):
        schur = blocks[k][k]
        for j in range(k):
            schur = schur - mul(lower[k][j], lower[k][j], True)
        lower[k][k], inverse = factor_block(schur)
        diag_inv.append(inverse)
        for i in range(k + 1, STEPS):
            below = blocks[i][k]
            for j in range(k):
                below = below - mul(lower[i][j], lower[k][j], True)
            lower[i][k] = mul(below, diag_inv[k], True)
    inv = [[None] * STEPS for _ in range(STEPS)]
    for i in range(STEPS):
        inv[i][i] = diag_inv[i]
        for j in range(i - 1, -1, -1):
            acc = mul(lower[i][j], inv[j][j])
            for m in range(j + 1, i):
                acc = acc + mul(lower[i][m], inv[m][j])
            inv[i][j] = -mul(diag_inv[i], acc)
    factor = jnp.concatenate(
        [jnp.concatenate([lower[i][j] if j <= i else zero for j in range(STEPS)], axis=1) for i in range(STEPS)], axis=0
    )
    inverse = jnp.concatenate(
        [jnp.concatenate([inv[i][j] if j <= i else zero for j in range(STEPS)], axis=1) for i in range(STEPS)], axis=0
    )
    return factor, inverse


def apply_inverse(band, inverse, axis):
    parts = []
    for j in range(STEPS):
        hi = (j + 1) * BLOCK
        piece = lax.slice_in_dim(band, 0, hi, axis=axis)
        parts.append(lax.dot_general(
            piece, inverse[j * BLOCK:hi, :hi], (((axis,), (1,)), ((), ())),
            precision=lax.Precision.HIGHEST, preferred_element_type=jnp.float32,
        ))
    return jnp.concatenate(parts, axis=1)


def shards(kernel):
    row_count = lax.axis_size("row")
    col_count = lax.axis_size("col")
    row_index = lax.axis_index("row")
    col_index = lax.axis_index("col")
    rows_local, cols_local = kernel.shape
    width = STEPS * BLOCK
    row_ids = jnp.arange(rows_local) // BLOCK * row_count + row_index
    col_ids = jnp.arange(cols_local) // BLOCK * col_count + col_index

    blocks = gather_corner(kernel, row_index, col_index)
    band_cols = gather_columns(kernel, col_index)
    band_rows = gather_rows(kernel, row_index)

    factor, inverse = factor_corner(blocks)
    panels = apply_inverse(band_cols, inverse, 1)
    across = apply_inverse(band_rows, inverse, 0)
    own = lax.dynamic_slice_in_dim(factor, jnp.minimum(row_index, STEPS - 1) * BLOCK, BLOCK, 0)
    own = jnp.pad(own, ((0, rows_local - BLOCK), (0, 0)))
    head = (jnp.arange(rows_local) < BLOCK)[:, None] & (row_index < STEPS)
    panels = jnp.where(head, own, panels)
    update = lax.dot_general(
        panels, across, (((1,), (1,)), ((), ())),
        precision=lax.Precision.HIGHEST, preferred_element_type=jnp.float32,
    )
    keep = (row_ids >= STEPS)[:, None] & (col_ids >= STEPS)[None, :]
    schur = jnp.where(keep, kernel - update, jnp.float32(0.0))
    return (schur, panels)


def solution(mesh):
    return jax.shard_map(
        shards,
        mesh=mesh,
        in_specs=(P("row", "col"),),
        out_specs=(P("row", "col"), P("row", None)),
        check_vma=False,
    )
```

```python
import jax
import jax.numpy as jnp
from jax import lax
from jax.sharding import PartitionSpec as P

BLOCK = 256
STEPS = 3


def pick(received, index, count, want):
    total = None
    for shift, part in enumerate(received):
        term = jnp.where((index - shift) % count == want, part, jnp.float32(0.0))
        total = term if total is None else total + term
    return total


def gather_corner(kernel, row_index, col_index):
    row_count = lax.axis_size("row")
    col_count = lax.axis_size("col")
    ring = 4
    rings = col_count // ring
    piece = kernel[:BLOCK, :BLOCK]
    heard = [piece]
    for shift in range(1, ring):
        pairs = [
            (a * col_count + b, a * col_count + (b + shift) % ring)
            for a in range(STEPS)
            for b in range(a + 1)
        ]
        heard.append(lax.ppermute(piece, ("row", "col"), pairs))
    bands = []
    for a in range(STEPS):
        band = jnp.concatenate([pick(heard, col_index % ring, ring, b) for b in range(a + 1)], axis=1)
        bands.append(jnp.pad(band, ((0, 0), (0, (STEPS - 1 - a) * BLOCK))))
    groups = [[0], list(range(1, STEPS))]
    blocks = [None] * STEPS
    for group in groups:
        width = (max(group) + 1) * BLOCK
        mine = None
        for a in group:
            term = jnp.where(row_index == a, bands[a][:, :width], jnp.float32(0.0))
            mine = term if mine is None else mine + term
        across = [mine]
        for hop in range(1, rings):
            pairs = [(a * col_count + z, a * col_count + hop * ring + z) for a in group for z in range(ring)]
            across.append(lax.ppermute(mine, ("row", "col"), pairs))
        mine = pick(across, col_index // ring, rings, 0)
        odd = row_index % 2 == 1
        held = mine
        for shift in range(1, row_count // 2):
            pairs = [
                (a * col_count + q, ((a + 2 * shift) % row_count) * col_count + q)
                for a in group
                for q in range(col_count)
            ]
            got = lax.ppermute(mine, ("row", "col"), pairs)
            source = 0 if len(group) == 1 else 2 - row_index % 2
            held = held + jnp.where((row_index - 2 * shift) % row_count == source, got, jnp.float32(0.0))
        pairs = [(p * col_count + q, (p ^ 1) * col_count + q) for p in range(row_count) for q in range(col_count)]
        other = lax.ppermute(held, ("row", "col"), pairs)
        for a in group:
            band = jnp.where(odd == (a % 2 == 1), held, other)
            blocks[a] = [band[:, b * BLOCK:(b + 1) * BLOCK] for b in range(a + 1)]
    return blocks


def gather_columns(kernel, col_index):
    rows = kernel.shape[0]
    mine = col_index < STEPS
    piece = jnp.where(mine, kernel[:, :BLOCK], jnp.float32(0.0))
    band = jnp.zeros((rows, STEPS * BLOCK), jnp.float32)
    band = lax.dynamic_update_slice(band, piece, (0, jnp.minimum(col_index, STEPS - 1) * BLOCK))
    return lax.psum(band, "col")


def gather_rows(kernel, row_index):
    cols = kernel.shape[1]
    mine = row_index < STEPS
    piece = jnp.where(mine, kernel[:BLOCK, :], jnp.float32(0.0))
    band = jnp.zeros((STEPS * BLOCK, cols), jnp.float32)
    band = lax.dynamic_update_slice(band, piece, (jnp.minimum(row_index, STEPS - 1) * BLOCK, 0))
    return lax.psum(band, "row")


def mul(a, b, transpose_b=False):
    dims = (((1,), (1 if transpose_b else 0,)), ((), ()))
    return lax.dot_general(a, b, dims, precision=lax.Precision.HIGHEST, preferred_element_type=jnp.float32)


def factor_block(schur):
    half = schur.shape[0] // 2
    eye = jnp.eye(half, dtype=jnp.float32)
    top = jnp.linalg.cholesky(schur[:half, :half])
    top_inv = jax.scipy.linalg.solve_triangular(top, eye, lower=True)
    side = mul(schur[half:, :half], top_inv, True)
    bottom = jnp.linalg.cholesky(schur[half:, half:] - mul(side, side, True))
    bottom_inv = jax.scipy.linalg.solve_triangular(bottom, eye, lower=True)
    corner = -mul(bottom_inv, mul(side, top_inv))
    zero = jnp.zeros((half, half), jnp.float32)
    factor = jnp.concatenate(
        [jnp.concatenate([top, zero], axis=1), jnp.concatenate([side, bottom], axis=1)], axis=0
    )
    inverse = jnp.concatenate(
        [jnp.concatenate([top_inv, zero], axis=1), jnp.concatenate([corner, bottom_inv], axis=1)], axis=0
    )
    return factor, inverse


def factor_corner(blocks):
    zero = jnp.zeros((BLOCK, BLOCK), jnp.float32)
    lower = [[None] * STEPS for _ in range(STEPS)]
    diag_inv = []
    for k in range(STEPS):
        schur = blocks[k][k]
        for j in range(k):
            schur = schur - mul(lower[k][j], lower[k][j], True)
        lower[k][k], inverse = factor_block(schur)
        diag_inv.append(inverse)
        for i in range(k + 1, STEPS):
            below = blocks[i][k]
            for j in range(k):
                below = below - mul(lower[i][j], lower[k][j], True)
            lower[i][k] = mul(below, diag_inv[k], True)
    inv = [[None] * STEPS for _ in range(STEPS)]
    for i in range(STEPS):
        inv[i][i] = diag_inv[i]
        for j in range(i - 1, -1, -1):
            acc = mul(lower[i][j], inv[j][j])
            for m in range(j + 1, i):
                acc = acc + mul(lower[i][m], inv[m][j])
            inv[i][j] = -mul(diag_inv[i], acc)
    factor = jnp.concatenate(
        [jnp.concatenate([lower[i][j] if j <= i else zero for j in range(STEPS)], axis=1) for i in range(STEPS)], axis=0
    )
    inverse = jnp.concatenate(
        [jnp.concatenate([inv[i][j] if j <= i else zero for j in range(STEPS)], axis=1) for i in range(STEPS)], axis=0
    )
    return factor, inverse


def apply_inverse(band, inverse, axis):
    parts = []
    for j in range(STEPS):
        hi = (j + 1) * BLOCK
        piece = lax.slice_in_dim(band, 0, hi, axis=axis)
        parts.append(lax.dot_general(
            piece, inverse[j * BLOCK:hi, :hi], (((axis,), (1,)), ((), ())),
            precision=lax.Precision.HIGHEST, preferred_element_type=jnp.float32,
        ))
    return jnp.concatenate(parts, axis=1)


def shards(kernel):
    row_count = lax.axis_size("row")
    col_count = lax.axis_size("col")
    row_index = lax.axis_index("row")
    col_index = lax.axis_index("col")
    rows_local, cols_local = kernel.shape
    width = STEPS * BLOCK
    row_ids = jnp.arange(rows_local) // BLOCK * row_count + row_index
    col_ids = jnp.arange(cols_local) // BLOCK * col_count + col_index

    blocks = gather_corner(kernel, row_index, col_index)
    band_cols = gather_columns(kernel, col_index)
    band_rows = gather_rows(kernel, row_index)

    factor, inverse = factor_corner(blocks)
    panels = apply_inverse(band_cols, inverse, 1)
    across = jnp.concatenate([
        lax.dot_general(
            inverse[j * BLOCK:(j + 1) * BLOCK, :(j + 1) * BLOCK], band_rows[:(j + 1) * BLOCK],
            (((1,), (0,)), ((), ())),
            precision=lax.Precision.HIGHEST, preferred_element_type=jnp.float32,
        )
        for j in range(STEPS)
    ], axis=0)
    own = lax.dynamic_slice_in_dim(factor, jnp.minimum(row_index, STEPS - 1) * BLOCK, BLOCK, 0)
    own = jnp.pad(own, ((0, rows_local - BLOCK), (0, 0)))
    head = (jnp.arange(rows_local) < BLOCK)[:, None] & (row_index < STEPS)
    panels = jnp.where(head, own, panels)
    update = lax.dot_general(
        panels, across, (((1,), (0,)), ((), ())),
        precision=lax.Precision.HIGHEST, preferred_element_type=jnp.float32,
    )
    keep = (row_ids >= STEPS)[:, None] & (col_ids >= STEPS)[None, :]
    schur = jnp.where(keep, kernel - update, jnp.float32(0.0))
    return (schur, panels)


def solution(mesh):
    return jax.shard_map(
        shards,
        mesh=mesh,
        in_specs=(P("row", "col"),),
        out_specs=(P("row", "col"), P("row", None)),
        check_vma=False,
    )
```

```python
import jax
import jax.numpy as jnp
from jax import lax
from jax.sharding import PartitionSpec as P

BLOCK = 256
STEPS = 3


def pick(received, index, count, want):
    total = None
    for shift, part in enumerate(received):
        term = jnp.where((index - shift) % count == want, part, jnp.float32(0.0))
        total = term if total is None else total + term
    return total


def gather_corner(kernel, row_index, col_index):
    row_count = lax.axis_size("row")
    col_count = lax.axis_size("col")
    ring = 4
    rings = col_count // ring
    piece = kernel[:BLOCK, :BLOCK]
    heard = [piece]
    for shift in range(1, ring):
        pairs = [
            (a * col_count + b, a * col_count + (b + shift) % ring)
            for a in range(STEPS)
            for b in range(a + 1)
        ]
        heard.append(lax.ppermute(piece, ("row", "col"), pairs))
    bands = []
    for a in range(STEPS):
        band = jnp.concatenate([pick(heard, col_index % ring, ring, b) for b in range(a + 1)], axis=1)
        bands.append(jnp.pad(band, ((0, 0), (0, (STEPS - 1 - a) * BLOCK))))
    groups = [[0], list(range(1, STEPS))]
    blocks = [None] * STEPS
    for group in groups:
        width = (max(group) + 1) * BLOCK
        mine = None
        for a in group:
            term = jnp.where(row_index == a, bands[a][:, :width], jnp.float32(0.0))
            mine = term if mine is None else mine + term
        across = [mine]
        for hop in range(1, rings):
            pairs = [(a * col_count + z, a * col_count + hop * ring + z) for a in group for z in range(ring)]
            across.append(lax.ppermute(mine, ("row", "col"), pairs))
        mine = pick(across, col_index // ring, rings, 0)
        odd = row_index % 2 == 1
        held = mine
        for shift in range(1, row_count // 2):
            pairs = [
                (a * col_count + q, ((a + 2 * shift) % row_count) * col_count + q)
                for a in group
                for q in range(col_count)
            ]
            got = lax.ppermute(mine, ("row", "col"), pairs)
            source = 0 if len(group) == 1 else 2 - row_index % 2
            held = held + jnp.where((row_index - 2 * shift) % row_count == source, got, jnp.float32(0.0))
        pairs = [(p * col_count + q, (p ^ 1) * col_count + q) for p in range(row_count) for q in range(col_count)]
        other = lax.ppermute(held, ("row", "col"), pairs)
        for a in group:
            band = jnp.where(odd == (a % 2 == 1), held, other)
            blocks[a] = [band[:, b * BLOCK:(b + 1) * BLOCK] for b in range(a + 1)]
    return blocks


def gather_columns(kernel, col_index):
    rows = kernel.shape[0]
    mine = col_index < STEPS
    piece = jnp.where(mine, kernel[:, :BLOCK], jnp.float32(0.0))
    band = jnp.zeros((rows, STEPS * BLOCK), jnp.float32)
    band = lax.dynamic_update_slice(band, piece, (0, jnp.minimum(col_index, STEPS - 1) * BLOCK))
    return lax.psum(band, "col")


def gather_rows(kernel, row_index):
    cols = kernel.shape[1]
    mine = row_index < STEPS
    piece = jnp.where(mine, kernel[:BLOCK, :], jnp.float32(0.0))
    band = jnp.zeros((STEPS * BLOCK, cols), jnp.float32)
    band = lax.dynamic_update_slice(band, piece, (jnp.minimum(row_index, STEPS - 1) * BLOCK, 0))
    return lax.psum(band, "row")


def mul(a, b, transpose_b=False):
    dims = (((1,), (1 if transpose_b else 0,)), ((), ()))
    return lax.dot_general(a, b, dims, precision=lax.Precision.HIGHEST, preferred_element_type=jnp.float32)


def factor_block(schur):
    half = schur.shape[0] // 2
    eye = jnp.eye(half, dtype=jnp.float32)
    top = lax.linalg.cholesky(schur[:half, :half], symmetrize_input=False)
    top_inv = jax.scipy.linalg.solve_triangular(top, eye, lower=True)
    side = mul(schur[half:, :half], top_inv, True)
    bottom = lax.linalg.cholesky(schur[half:, half:] - mul(side, side, True), symmetrize_input=False)
    bottom_inv = jax.scipy.linalg.solve_triangular(bottom, eye, lower=True)
    corner = -mul(bottom_inv, mul(side, top_inv))
    zero = jnp.zeros((half, half), jnp.float32)
    factor = jnp.concatenate(
        [jnp.concatenate([top, zero], axis=1), jnp.concatenate([side, bottom], axis=1)], axis=0
    )
    inverse = jnp.concatenate(
        [jnp.concatenate([top_inv, zero], axis=1), jnp.concatenate([corner, bottom_inv], axis=1)], axis=0
    )
    return factor, inverse


def factor_corner(blocks):
    zero = jnp.zeros((BLOCK, BLOCK), jnp.float32)
    lower = [[None] * STEPS for _ in range(STEPS)]
    diag_inv = []
    for k in range(STEPS):
        schur = blocks[k][k]
        for j in range(k):
            schur = schur - mul(lower[k][j], lower[k][j], True)
        lower[k][k], inverse = factor_block(schur)
        diag_inv.append(inverse)
        for i in range(k + 1, STEPS):
            below = blocks[i][k]
            for j in range(k):
                below = below - mul(lower[i][j], lower[k][j], True)
            lower[i][k] = mul(below, diag_inv[k], True)
    inv = [[None] * STEPS for _ in range(STEPS)]
    for i in range(STEPS):
        inv[i][i] = diag_inv[i]
        for j in range(i - 1, -1, -1):
            acc = mul(lower[i][j], inv[j][j])
            for m in range(j + 1, i):
                acc = acc + mul(lower[i][m], inv[m][j])
            inv[i][j] = -mul(diag_inv[i], acc)
    factor = jnp.concatenate(
        [jnp.concatenate([lower[i][j] if j <= i else zero for j in range(STEPS)], axis=1) for i in range(STEPS)], axis=0
    )
    inverse = jnp.concatenate(
        [jnp.concatenate([inv[i][j] if j <= i else zero for j in range(STEPS)], axis=1) for i in range(STEPS)], axis=0
    )
    return factor, inverse


def apply_inverse(band, inverse, axis):
    parts = []
    for j in range(STEPS):
        hi = (j + 1) * BLOCK
        piece = lax.slice_in_dim(band, 0, hi, axis=axis)
        parts.append(lax.dot_general(
            piece, inverse[j * BLOCK:hi, :hi], (((axis,), (1,)), ((), ())),
            precision=lax.Precision.HIGHEST, preferred_element_type=jnp.float32,
        ))
    return jnp.concatenate(parts, axis=1)


def shards(kernel):
    row_count = lax.axis_size("row")
    col_count = lax.axis_size("col")
    row_index = lax.axis_index("row")
    col_index = lax.axis_index("col")
    rows_local, cols_local = kernel.shape
    width = STEPS * BLOCK
    row_ids = jnp.arange(rows_local) // BLOCK * row_count + row_index
    col_ids = jnp.arange(cols_local) // BLOCK * col_count + col_index

    blocks = gather_corner(kernel, row_index, col_index)
    band_cols = gather_columns(kernel, col_index)
    band_rows = gather_rows(kernel, row_index)

    factor, inverse = factor_corner(blocks)
    panels = apply_inverse(band_cols, inverse, 1)
    across = jnp.concatenate([
        lax.dot_general(
            inverse[j * BLOCK:(j + 1) * BLOCK, :(j + 1) * BLOCK], band_rows[:(j + 1) * BLOCK],
            (((1,), (0,)), ((), ())),
            precision=lax.Precision.HIGHEST, preferred_element_type=jnp.float32,
        )
        for j in range(STEPS)
    ], axis=0)
    own = lax.dynamic_slice_in_dim(factor, jnp.minimum(row_index, STEPS - 1) * BLOCK, BLOCK, 0)
    own = jnp.pad(own, ((0, rows_local - BLOCK), (0, 0)))
    head = (jnp.arange(rows_local) < BLOCK)[:, None] & (row_index < STEPS)
    panels = jnp.where(head, own, panels)
    update = lax.dot_general(
        panels, across, (((1,), (0,)), ((), ())),
        precision=lax.Precision.HIGHEST, preferred_element_type=jnp.float32,
    )
    keep = (row_ids >= STEPS)[:, None] & (col_ids >= STEPS)[None, :]
    schur = jnp.where(keep, kernel - update, jnp.float32(0.0))
    return (schur, panels)


def solution(mesh):
    return jax.shard_map(
        shards,
        mesh=mesh,
        in_specs=(P("row", "col"),),
        out_specs=(P("row", "col"), P("row", None)),
        check_vma=False,
    )
```
